256 devices in a mesh: tok: 64 (over z, x, core), mlp: 4 (over y).
Axes of the slice: x: 4, y: 4, z: 8, core: 2. Of those that a mesh axis runs over, the one named last changes fastest.
Arguments:
- new_x: bfloat16 [16, 512, 8192], P(None, ('tok', 'mlp')), may hold values from -6 to 6
- gate_input: bfloat16 [16, 512, 8192], P(None, ('tok', 'mlp')), may hold values from -40 to 40
- state_proj: bfloat16 [16, 512, 8, 256], P(None, ('tok', 'mlp')), may hold values from -1.796875 to 1.796875
- step_size: float32 [16, 512, 128], P('mlp', None, 'tok'), may hold values from 0.25 to 4
- decay_rate: float32 [128], P('tok'), may hold values from -12 to -3
- x_cache: bfloat16 [16, 3072, 8192], P('mlp', None, 'tok'), may hold values from -6 to 6
- b_cache: bfloat16 [16, 8, 3072, 128], P('mlp', None, 'tok'), may hold values from -1.8 to 1.8
- decay_cache: float32 [16, 128, 3072], P('mlp', 'tok'), may hold values from -1 to 0
- lengths: int32 [16], P('mlp'), may hold values from 64 to 3072, as said below
- sink_pos: int32 [16, 4], P('mlp'), may hold values from 0 to 63, as said below
- windows: int32 [16], P('mlp'), may hold values from 1024 to 2048, as said below
- norm_gain: float32 [8192], replicated, may hold values from 0.5 to 1.5
Outputs:
- mixer_normed: bfloat16 [16, 512, 8192], P(None, ('tok', 'mlp'))
The draws below stay inside these ranges and needn't reach their ends.
Inputs may be any that keep to these rules, and one draw needn't show every extreme that they name: `lengths`: some request holds exactly 3072 cached positions. `windows`: some request has a window of exactly 2048. `sink_pos`: a request's sink positions increase and lie below its length.
All inputs are finite; a program needn't handle non-finite values.
Results may differ from the reference program's by a relative error of at most 0.0061.
Values may be sent and summed in bfloat16 or wider, within the bound.
No kernel may reach another device: no remote copies, remote signals or barrier semaphores. Data moves between devices by JAX's collectives and lax.ppermute only.
A program may use at most 64 MiB of HBM per device.

```python
import math
import jax
import jax.numpy as jnp
from jax import lax

MIXER_HEADS = 128
HEAD_DIM = 64
GROUPS = 8
STATE = 128
NEW = 512
CACHE_CAPACITY = 3072
WINDOW_LIMIT = 2048
SINKS = 4
REQUEST_TOTAL = 16


def head_rates(key):
    pick_key, slow_key, fast_key = jax.random.split(jax.random.fold_in(key, 5), 3)
    slow_share = 0.5
    slow_mask = jax.random.uniform(pick_key, (MIXER_HEADS,)) < slow_share
    slow_rate = jax.random.uniform(slow_key, (MIXER_HEADS,), minval=0.05, maxval=0.3) / WINDOW_LIMIT
    fast_rate = jax.random.uniform(fast_key, (MIXER_HEADS,), minval=1.5, maxval=3.0) / WINDOW_LIMIT
    return jnp.where(slow_mask, slow_rate, fast_rate)


def draw_decay_rate(key, part):
    return jnp.log(head_rates(key)).astype(jnp.float32)


def draw_decay_cache(key, part):
    head_decay_values = head_rates(key)
    rough_random_key, spike_random_key, depth_random_key = jax.random.split(jax.random.fold_in(key, 9), 3)
    rough_values = jax.random.uniform(rough_random_key, (REQUEST_TOTAL, MIXER_HEADS, CACHE_CAPACITY), minval=0.5, maxval=1.5)
    decay_spikes = jax.random.uniform(spike_random_key, (REQUEST_TOTAL, MIXER_HEADS, CACHE_CAPACITY)) < 3.0 / WINDOW_LIMIT
    cache_depth = jnp.log(jax.random.uniform(depth_random_key, (REQUEST_TOTAL, MIXER_HEADS, CACHE_CAPACITY), minval=0.5, maxval=0.8))
    return (-head_decay_values[None, :, None] * rough_values + jnp.where(decay_spikes, cache_depth, 0.0)).astype(jnp.float32)


def draw_b_cache(key, part):
    inner_key = jax.random.fold_in(key, 13)
    base = jnp.clip(jax.random.normal(inner_key, (REQUEST_TOTAL, GROUPS, CACHE_CAPACITY, STATE)), -6.0, 6.0) * 0.3
    return base.astype(jnp.bfloat16)


def draw_gate_input(key, part):
    base_key, row_key, col_key = jax.random.split(jax.random.fold_in(key, 17), 3)
    shape = (REQUEST_TOTAL, NEW, MIXER_HEADS * HEAD_DIM)
    base = jnp.clip(jax.random.normal(base_key, shape), -4.0, 4.0)
    rows = jnp.exp(jax.random.uniform(row_key, (REQUEST_TOTAL, NEW, 1), minval=-1.15, maxval=1.15))
    cols = jnp.exp(jax.random.uniform(col_key, (1, 1, MIXER_HEADS * HEAD_DIM), minval=-1.15, maxval=1.15))
    return (base * rows * cols).astype(jnp.bfloat16)


def draw_lengths(key, part):
    value_key, top_key = jax.random.split(jax.random.fold_in(key, 21))
    values = jax.random.randint(value_key, (REQUEST_TOTAL,), 16 * SINKS, CACHE_CAPACITY + 1)
    longest = jax.random.randint(top_key, (), 0, REQUEST_TOTAL)
    return jnp.where(jnp.arange(REQUEST_TOTAL) == longest, CACHE_CAPACITY, values).astype(jnp.int32)


def draw_windows(key, part):
    value_key, top_key = jax.random.split(jax.random.fold_in(key, 25))
    values = jax.random.randint(value_key, (REQUEST_TOTAL,), WINDOW_LIMIT // 2, WINDOW_LIMIT + 1)
    widest = jax.random.randint(top_key, (), 0, REQUEST_TOTAL)
    return jnp.where(jnp.arange(REQUEST_TOTAL) == widest, WINDOW_LIMIT, values).astype(jnp.int32)


def draw_sink_pos(key, part):
    offsets = jax.random.randint(jax.random.fold_in(key, 29), (REQUEST_TOTAL, SINKS), 0, 16)
    return (16 * jnp.arange(SINKS, dtype=jnp.int32)[None, :] + offsets).astype(jnp.int32)


def steps_of(own_key, shape, pieces, smallest, high):
    level, own = 1.0, jax.random.fold_in(own_key, 6)
    for dim, blocks in pieces:
        draws = jnp.exp(jax.random.uniform(jax.random.fold_in(own, dim), (blocks,), jnp.float32, smallest / len(pieces), high / len(pieces)))
        level = level * jnp.repeat(draws, shape[dim] // blocks).reshape([-1 if axis == dim else 1 for axis in range(len(shape))])
    return level


def centred(stream_key, shape, width, bound, pieces=(), kind=jnp.bfloat16):
    drawn = jax.random.normal(stream_key, shape, jnp.float32) * width
    if len(pieces) > 0:
        drawn = steps_of(stream_key, shape, pieces, -0.22, 0.18) * drawn
    return jnp.clip(drawn, min=-bound, max=bound).astype(kind)


def setup_inputs(seed: int = 0) -> dict:
    key_of = jax.random.split(jax.random.key(seed), 13)
    new_x = centred(key_of[0], (REQUEST_TOTAL, NEW, MIXER_HEADS * HEAD_DIM), 1.0, 6.0, ((1, 256),))
    gate_input = draw_gate_input(jax.random.fold_in(key_of[12], 71), 0)
    state_proj = centred(key_of[2], (REQUEST_TOTAL, NEW, GROUPS, 2 * STATE), 0.3, 1.796875, ((1, 256),))
    step_size = jnp.clip(jnp.exp(math.log(4.0) - 2.7725887 * jax.random.uniform(key_of[3], (REQUEST_TOTAL, NEW, MIXER_HEADS), jnp.float32) ** steps_of(key_of[3], (REQUEST_TOTAL, NEW, MIXER_HEADS), ((0, 4), (2, 64)), -0.2, 0.2)), 0.25, 4.0)
    decay_rate = draw_decay_rate(jax.random.fold_in(key_of[12], 71), 0)
    x_cache = centred(key_of[5], (REQUEST_TOTAL, CACHE_CAPACITY, MIXER_HEADS * HEAD_DIM), 1.0, 6.0, ((0, 4), (2, 64)))
    b_cache = draw_b_cache(jax.random.fold_in(key_of[12], 71), 0)
    decay_cache = draw_decay_cache(jax.random.fold_in(key_of[12], 71), 0)
    lengths = draw_lengths(jax.random.fold_in(key_of[12], 71), 0)
    sink_pos = draw_sink_pos(jax.random.fold_in(key_of[12], 71), 0)
    windows = draw_windows(jax.random.fold_in(key_of[12], 71), 0)
    norm_gain = jnp.clip(1.0 + 0.1 * jax.random.normal(key_of[11], (MIXER_HEADS * HEAD_DIM,), jnp.float32), 0.5, 1.5)
    return dict(new_x=new_x, gate_input=gate_input, state_proj=state_proj, step_size=step_size, decay_rate=decay_rate, x_cache=x_cache, b_cache=b_cache, decay_cache=decay_cache, lengths=lengths, sink_pos=sink_pos, windows=windows, norm_gain=norm_gain)


EPS = 1e-05

def request_output(request_parts):
    cum_new, scaled_x, state_now, cache_x, decay_now, cache_b, length, sink_now, window = request_parts
    cache_pos = jnp.arange(CACHE_CAPACITY, dtype=jnp.int32)
    new_pos = jnp.arange(NEW, dtype=jnp.int32)
    live_mask = cache_pos < length
    masked = jnp.where(live_mask[None, :], decay_now, jnp.float32(0.0))
    cache_cum = jnp.cumsum(masked, axis=1)
    tail_sum = cache_cum[:, -1:] - cache_cum
    cache_gap = (length + new_pos)[:, None] - cache_pos[None, :]
    in_window = (cache_gap < window) & live_mask[None, :]
    sink_hit = jnp.any(cache_pos[None, :] == sink_now[:, None], axis=0) & live_mask
    sink_only = sink_hit[None, :] & jnp.logical_not(in_window)
    new_gap = new_pos[:, None] - new_pos[None, :]
    new_keep = (new_gap >= 0) & (new_gap < window)
    per_group = MIXER_HEADS // GROUPS

    def group_output(group_index):
        group_state = lax.dynamic_index_in_dim(state_now, group_index, 1, keepdims=False)
        b_new = group_state[:, :STATE]
        c_now = group_state[:, STATE:]
        b_old = lax.dynamic_index_in_dim(cache_b, group_index, 0, keepdims=False)
        score_old = jnp.dot(c_now, b_old.T, preferred_element_type=jnp.float32)
        score_new = jnp.dot(c_now, b_new.T, preferred_element_type=jnp.float32)

        def head_output(offset):
            head_index = group_index * per_group + offset
            tail_head = lax.dynamic_index_in_dim(tail_sum, head_index, 0, keepdims=False)
            cum_head = lax.dynamic_index_in_dim(cum_new, head_index, 1, keepdims=False)
            decay_old = jnp.exp(jnp.minimum(cum_head[:, None] + tail_head[None, :], 0.0))
            weight_old = jnp.where(in_window, decay_old, jnp.where(sink_only, 1.0, 0.0))
            decay_new = jnp.exp(jnp.minimum(cum_head[:, None] - cum_head[None, :], 0.0))
            weight_new = jnp.where(new_keep, decay_new, 0.0)
            probs_old = (score_old * weight_old).astype(jnp.bfloat16)
            probs_new = (score_new * weight_new).astype(jnp.bfloat16)
            x_old = lax.dynamic_slice_in_dim(cache_x, head_index * HEAD_DIM, HEAD_DIM, 1)
            x_new = lax.dynamic_slice_in_dim(scaled_x, head_index * HEAD_DIM, HEAD_DIM, 1)
            return jnp.dot(probs_old, x_old, preferred_element_type=jnp.float32) + jnp.dot(probs_new, x_new, preferred_element_type=jnp.float32)
        head_outs = lax.map(head_output, jnp.arange(per_group, dtype=jnp.int32))
        return jnp.transpose(head_outs, (1, 0, 2)).reshape(NEW, per_group * HEAD_DIM)
    group_outs = lax.map(group_output, jnp.arange(GROUPS, dtype=jnp.int32))
    return jnp.transpose(group_outs, (1, 0, 2)).reshape(NEW, MIXER_HEADS * HEAD_DIM)

def reference(new_x, gate_input, state_proj, step_size, decay_rate, x_cache, b_cache, decay_cache, lengths, sink_pos, windows, norm_gain):
    log_decay = -(step_size * jnp.exp(decay_rate)[None, None, :])
    cum_new = jnp.cumsum(log_decay, axis=1)
    scaled_x = new_x.astype(jnp.float32).reshape(REQUEST_TOTAL, NEW, MIXER_HEADS, HEAD_DIM) * step_size[..., None]
    scaled_x = scaled_x.reshape(REQUEST_TOTAL, NEW, MIXER_HEADS * HEAD_DIM).astype(jnp.bfloat16)
    mixer_out = lax.map(request_output, (cum_new, scaled_x, state_proj, x_cache, decay_cache, b_cache, lengths, sink_pos, windows))
    mixer_out = lax.optimization_barrier(mixer_out.astype(jnp.bfloat16))
    gated_out = mixer_out.astype(jnp.float32) * jax.nn.silu(gate_input.astype(jnp.float32))
    grouped = gated_out.reshape(REQUEST_TOTAL, NEW, GROUPS, -1)
    norm_scale = lax.rsqrt(lax.optimization_barrier(jnp.mean(grouped * grouped, axis=-1, keepdims=True)) + EPS)
    normed = (grouped * norm_scale).reshape(REQUEST_TOTAL, NEW, MIXER_HEADS * HEAD_DIM) * norm_gain
    return normed.astype(jnp.bfloat16)
```

```python
import jax
import jax.numpy as jnp
from jax import lax
from jax.sharding import PartitionSpec as P

EPS = 1e-05


def per_device(
    new_x,
    gate_input,
    state_proj,
    step_size,
    decay_rate,
    x_cache,
    b_cache,
    decay_cache,
    lengths,
    sink_pos,
    windows,
    norm_gain,
):
    n_tok = lax.axis_size("tok")
    n_mlp = lax.axis_size("mlp")
    n_dev = n_tok * n_mlp
    groups = state_proj.shape[2]
    state_dim = b_cache.shape[3]
    copies = n_tok // groups
    heads_dev = decay_rate.shape[0]
    requests = step_size.shape[0]
    new_len = step_size.shape[1]
    tok_blk = new_x.shape[1]
    cache_len = x_cache.shape[1]
    chans = x_cache.shape[2]
    head_dim = chans // heads_dev

    x_part = new_x.reshape(n_mlp, requests, tok_blk, n_tok, chans).transpose(3, 0, 1, 2, 4)
    sp = state_proj.reshape(n_mlp, requests, tok_blk, groups, 2 * state_dim)
    sp = jnp.repeat(sp, copies, axis=3).transpose(3, 0, 1, 2, 4)
    packed = jnp.concatenate([x_part, sp], axis=-1).reshape(n_dev, requests, tok_blk, -1)
    got = lax.all_to_all(packed, ("tok", "mlp"), 0, 0, tiled=True)
    got = got.transpose(1, 0, 2, 3).reshape(requests, new_len, -1)
    head_x = got[..., :chans]
    b_new = got[..., chans : chans + state_dim]
    c_now = got[..., chans + state_dim :]

    shared_b = lax.all_to_all(
        jnp.repeat(b_cache, copies, axis=1), "tok", split_axis=1, concat_axis=2, tiled=True
    )[:, 0]

    head_decay_values = jnp.exp(decay_rate)
    cum_new = jnp.cumsum(-(step_size * head_decay_values), axis=1)
    scaled = head_x.astype(jnp.float32).reshape(requests, new_len, heads_dev, head_dim)
    scaled = (scaled * step_size[..., None]).astype(jnp.bfloat16)

    positions = jnp.arange(cache_len, dtype=jnp.int32)
    token_order = jnp.arange(new_len, dtype=jnp.int32)
    live = positions[None, :] < lengths[:, None]
    masked = jnp.where(live[:, None, :], decay_cache, 0.0)
    local_sum = jnp.cumsum(masked, axis=2)
    tail_sum = local_sum[:, :, -1:] - local_sum

    col_scale = jnp.exp(tail_sum)
    row_scale = jnp.exp(cum_new)
    x_scaled = x_cache.astype(jnp.float32).reshape(requests, cache_len, heads_dev, head_dim)
    x_scaled = x_scaled * col_scale.transpose(0, 2, 1)[..., None]
    x_scaled = x_scaled.reshape(requests, cache_len, chans)
    x_hi = x_scaled.astype(jnp.bfloat16)
    x_lo = (x_scaled - x_hi.astype(jnp.float32)).astype(jnp.bfloat16)
    x_pair = jnp.concatenate([x_hi, x_lo], axis=-1)

    query_pos = lengths[:, None] + token_order[None, :]
    in_window = (query_pos[:, :, None] - positions[None, None, :] < windows[:, None, None]) & live[
        :, None, :
    ]
    score_old = jnp.einsum("rnk,rsk->rns", c_now, shared_b, preferred_element_type=jnp.float32)
    probs_old = jnp.where(in_window, score_old, 0.0).astype(jnp.bfloat16)
    acc = jnp.einsum("rns,rsc->rnc", probs_old, x_pair, preferred_element_type=jnp.float32)
    old_out = (acc[..., :chans] + acc[..., chans:]).reshape(requests, new_len, heads_dev, head_dim)
    old_out = old_out * row_scale[..., None]

    sink_b = jnp.take_along_axis(shared_b, sink_pos[:, :, None], axis=1)
    sink_x = jnp.take_along_axis(x_cache, sink_pos[:, :, None], axis=1)
    sink_live = sink_pos < lengths[:, None]
    sink_gap = query_pos[:, :, None] - sink_pos[:, None, :]
    sink_only = sink_live[:, None, :] & jnp.logical_not(sink_gap < windows[:, None, None])
    score_sink = jnp.einsum("rnk,rjk->rnj", c_now, sink_b, preferred_element_type=jnp.float32)
    probs_sink = jnp.where(sink_only, score_sink, 0.0).astype(jnp.bfloat16)
    sink_out = jnp.einsum("rnj,rjc->rnc", probs_sink, sink_x, preferred_element_type=jnp.float32)

    score_new = jnp.einsum("rnk,rjk->rnj", c_now, b_new, preferred_element_type=jnp.float32)
    new_gap = token_order[:, None] - token_order[None, :]
    keep_new = (new_gap[None] >= 0) & (new_gap[None] < windows[:, None, None])
    cum_t = cum_new.transpose(0, 2, 1)
    decay_new = jnp.exp(jnp.minimum(cum_t[:, :, :, None] - cum_t[:, :, None, :], 0.0))
    weight_new = jnp.where(keep_new[:, None], decay_new, 0.0)
    probs_new = (score_new[:, None] * weight_new).astype(jnp.bfloat16)
    new_out = jnp.einsum("rhnj,rjhd->rnhd", probs_new, scaled, preferred_element_type=jnp.float32)

    mixer_out = (old_out + new_out).reshape(requests, new_len, chans) + sink_out
    mixer_out = mixer_out.astype(jnp.bfloat16)

    back = mixer_out.reshape(requests, n_dev, tok_blk, chans).transpose(1, 0, 2, 3)
    back = lax.all_to_all(back, ("tok", "mlp"), 0, 0, tiled=True)
    back = back.reshape(n_tok, n_mlp, requests, tok_blk, chans).transpose(1, 2, 3, 0, 4)
    mixer_tok = lax.optimization_barrier(back.reshape(n_mlp * requests, tok_blk, n_tok * chans))

    gated_out = mixer_tok.astype(jnp.float32) * jax.nn.silu(gate_input.astype(jnp.float32))
    grouped = gated_out.reshape(gated_out.shape[0], gated_out.shape[1], groups, -1)
    norm_scale = lax.rsqrt(jnp.mean(grouped * grouped, axis=-1, keepdims=True) + EPS)
    normed = (grouped * norm_scale).reshape(gated_out.shape) * norm_gain
    return normed.astype(jnp.bfloat16)


def solution(mesh):
    return jax.shard_map(
        per_device,
        mesh=mesh,
        in_specs=(
            P(None, ("tok", "mlp"), None),
            P(None, ("tok", "mlp"), None),
            P(None, ("tok", "mlp"), None, None),
            P("mlp", None, "tok"),
            P("tok"),
            P("mlp", None, "tok"),
            P("mlp", None, "tok", None),
            P("mlp", "tok", None),
            P("mlp"),
            P("mlp", None),
            P("mlp"),
            P(),
        ),
        out_specs=P(None, ("tok", "mlp"), None),
        check_vma=False,
    )
```

```python
import jax
import jax.numpy as jnp
from jax import lax
from jax.sharding import Mesh, PartitionSpec as P

EPS = 1e-05
GROUPS = 8


def per_device(
    new_x,
    gate_input,
    state_proj,
    step_size,
    decay_rate,
    x_cache,
    b_cache,
    decay_cache,
    lengths,
    sink_pos,
    windows,
    norm_gain,
):
    n_tz = lax.axis_size("tz")
    n_txc = lax.axis_size("txc")
    n_tok = n_tz * n_txc
    n_mlp = lax.axis_size("mlp")
    n_dev = n_tok * n_mlp
    groups = state_proj.shape[2]
    state_dim = b_cache.shape[3]
    heads_dev = decay_rate.shape[0]
    requests = step_size.shape[0]
    new_len = step_size.shape[1]
    tok_blk = new_x.shape[1]
    cache_len = x_cache.shape[1]
    chans = x_cache.shape[2]
    head_dim = chans // heads_dev

    part_b = lax.all_to_all(b_cache, "tz", split_axis=1, concat_axis=1, tiled=True)
    shared_b = lax.all_gather(part_b, "txc", axis=2)
    shared_b = shared_b.reshape(requests, cache_len, state_dim)

    sp = state_proj.reshape(n_mlp, requests, tok_blk, groups, 2 * state_dim)
    sp = sp.transpose(3, 0, 1, 2, 4).reshape(groups * n_mlp, requests, tok_blk, -1)
    sp = lax.all_to_all(sp, ("tz", "mlp"), 0, 0, tiled=True)
    sp = lax.all_gather(sp, "txc", axis=1)
    sp = sp.reshape(n_tz, n_mlp, n_txc, requests, tok_blk, -1).transpose(3, 0, 2, 1, 4, 5)
    sp = sp.reshape(requests, new_len, -1)
    b_new = sp[..., :state_dim]
    c_now = sp[..., state_dim:]

    x_part = new_x.reshape(n_mlp, requests, tok_blk, n_tok, chans).transpose(3, 0, 1, 2, 4)
    x_part = x_part.reshape(n_dev, requests, tok_blk, chans)
    head_x = lax.all_to_all(x_part, ("tz", "txc", "mlp"), 0, 0, tiled=True)
    head_x = head_x.transpose(1, 0, 2, 3).reshape(requests, new_len, chans)

    head_decay_values = jnp.exp(decay_rate)
    cum_new = jnp.cumsum(-(step_size * head_decay_values), axis=1)
    scaled = head_x.astype(jnp.float32).reshape(requests, new_len, heads_dev, head_dim)
    scaled = (scaled * step_size[..., None]).astype(jnp.bfloat16)

    positions = jnp.arange(cache_len, dtype=jnp.int32)
    token_order = jnp.arange(new_len, dtype=jnp.int32)
    live = positions[None, :] < lengths[:, None]
    masked = jnp.where(live[:, None, :], decay_cache, 0.0)
    local_sum = jnp.cumsum(masked, axis=2)
    tail_sum = local_sum[:, :, -1:] - local_sum

    col_scale = jnp.exp(tail_sum)
    row_scale = jnp.exp(cum_new)
    x_scaled = x_cache.astype(jnp.float32).reshape(requests, cache_len, heads_dev, head_dim)
    x_scaled = x_scaled * col_scale.transpose(0, 2, 1)[..., None]
    x_scaled = x_scaled.reshape(requests, cache_len, chans)
    x_hi = x_scaled.astype(jnp.bfloat16)
    x_lo = (x_scaled - x_hi.astype(jnp.float32)).astype(jnp.bfloat16)
    x_pair = jnp.concatenate([x_hi, x_lo], axis=-1)

    query_pos = lengths[:, None] + token_order[None, :]
    in_window = (query_pos[:, :, None] - positions[None, None, :] < windows[:, None, None]) & live[
        :, None, :
    ]
    score_old = jnp.einsum("rnk,rsk->rns", c_now, shared_b, preferred_element_type=jnp.float32)
    probs_old = jnp.where(in_window, score_old, 0.0).astype(jnp.bfloat16)
    acc = jnp.einsum("rns,rsc->rnc", probs_old, x_pair, preferred_element_type=jnp.float32)
    old_out = (acc[..., :chans] + acc[..., chans:]).reshape(requests, new_len, heads_dev, head_dim)
    old_out = old_out * row_scale[..., None]

    sink_b = jnp.take_along_axis(shared_b, sink_pos[:, :, None], axis=1)
    sink_x = jnp.take_along_axis(x_cache, sink_pos[:, :, None], axis=1)
    sink_live = sink_pos < lengths[:, None]
    sink_gap = query_pos[:, :, None] - sink_pos[:, None, :]
    sink_only = sink_live[:, None, :] & jnp.logical_not(sink_gap < windows[:, None, None])
    score_sink = jnp.einsum("rnk,rjk->rnj", c_now, sink_b, preferred_element_type=jnp.float32)
    probs_sink = jnp.where(sink_only, score_sink, 0.0).astype(jnp.bfloat16)
    sink_out = jnp.einsum("rnj,rjc->rnc", probs_sink, sink_x, preferred_element_type=jnp.float32)

    score_new = jnp.einsum("rnk,rjk->rnj", c_now, b_new, preferred_element_type=jnp.float32)
    new_gap = token_order[:, None] - token_order[None, :]
    keep_new = (new_gap[None] >= 0) & (new_gap[None] < windows[:, None, None])
    cum_t = cum_new.transpose(0, 2, 1)
    decay_new = jnp.exp(jnp.minimum(cum_t[:, :, :, None] - cum_t[:, :, None, :], 0.0))
    weight_new = jnp.where(keep_new[:, None], decay_new, 0.0)
    probs_new = (score_new[:, None] * weight_new).astype(jnp.bfloat16)
    new_out = jnp.einsum("rhnj,rjhd->rnhd", probs_new, scaled, preferred_element_type=jnp.float32)

    mixer_out = (old_out + new_out).reshape(requests, new_len, chans) + sink_out
    mixer_out = mixer_out.astype(jnp.bfloat16)

    back = mixer_out.reshape(requests, n_dev, tok_blk, chans).transpose(1, 0, 2, 3)
    back = lax.all_to_all(back, ("tz", "txc", "mlp"), 0, 0, tiled=True)
    back = back.reshape(n_tok, n_mlp, requests, tok_blk, chans).transpose(1, 2, 3, 0, 4)
    mixer_tok = lax.optimization_barrier(back.reshape(n_mlp * requests, tok_blk, n_tok * chans))

    gated_out = mixer_tok.astype(jnp.float32) * jax.nn.silu(gate_input.astype(jnp.float32))
    grouped = gated_out.reshape(gated_out.shape[0], gated_out.shape[1], groups, -1)
    norm_scale = lax.rsqrt(jnp.mean(grouped * grouped, axis=-1, keepdims=True) + EPS)
    normed = (grouped * norm_scale).reshape(gated_out.shape) * norm_gain
    return normed.astype(jnp.bfloat16)


def solution(mesh):
    n_tok, n_mlp = mesh.shape["tok"], mesh.shape["mlp"]
    split = Mesh(mesh.devices.reshape(GROUPS, n_tok // GROUPS, n_mlp), ("tz", "txc", "mlp"))
    tok = ("tz", "txc")
    return jax.shard_map(
        per_device,
        mesh=split,
        in_specs=(
            P(None, (*tok, "mlp"), None),
            P(None, (*tok, "mlp"), None),
            P(None, (*tok, "mlp"), None, None),
            P("mlp", None, tok),
            P(tok),
            P("mlp", None, tok),
            P("mlp", None, tok, None),
            P("mlp", tok, None),
            P("mlp"),
            P("mlp", None),
            P("mlp"),
            P(),
        ),
        out_specs=P(None, (*tok, "mlp"), None),
        check_vma=False,
    )
```

```python
import jax
import jax.numpy as jnp
from jax import lax
from jax.sharding import Mesh, PartitionSpec as P

EPS = 1e-05
GROUPS = 8


def per_device(
    new_x,
    gate_input,
    state_proj,
    step_size,
    decay_rate,
    x_cache,
    b_cache,
    decay_cache,
    lengths,
    sink_pos,
    windows,
    norm_gain,
):
    n_tz = lax.axis_size("tz")
    n_txc = lax.axis_size("txc")
    n_tok = n_tz * n_txc
    n_mlp = lax.axis_size("mlp")
    n_dev = n_tok * n_mlp
    groups = state_proj.shape[2]
    state_dim = b_cache.shape[3]
    heads_dev = decay_rate.shape[0]
    requests = step_size.shape[0]
    new_len = step_size.shape[1]
    tok_blk = new_x.shape[1]
    cache_len = x_cache.shape[1]
    chans = x_cache.shape[2]
    head_dim = chans // heads_dev

    part_b = lax.all_to_all(b_cache, "tz", split_axis=1, concat_axis=1, tiled=True)
    sp = state_proj.reshape(n_mlp, requests, tok_blk, groups, 2 * state_dim)
    sp = sp.transpose(3, 0, 1, 2, 4).reshape(groups * n_mlp, requests, tok_blk, -1)
    sp = lax.all_to_all(sp, ("tz", "mlp"), 0, 0, tiled=True)
    packed = jnp.concatenate([part_b.reshape(-1), sp.reshape(-1)])
    packed = lax.all_gather(packed, "txc")
    b_size = part_b.size
    shared_b = packed[:, :b_size].reshape(n_txc, requests, n_tz, -1, state_dim)
    shared_b = shared_b.transpose(1, 2, 0, 3, 4).reshape(requests, cache_len, state_dim)
    sp = packed[:, b_size:].reshape(n_txc, n_tz, n_mlp, requests, tok_blk, -1)
    sp = sp.transpose(3, 1, 0, 2, 4, 5).reshape(requests, new_len, -1)
    b_new = sp[..., :state_dim]
    c_now = sp[..., state_dim:]

    x_part = new_x.reshape(n_mlp, requests, tok_blk, n_tok, chans).transpose(3, 0, 1, 2, 4)
    x_part = x_part.reshape(n_dev, requests, tok_blk, chans)
    head_x = lax.all_to_all(x_part, ("tz", "txc", "mlp"), 0, 0, tiled=True)
    head_x = head_x.transpose(1, 0, 2, 3).reshape(requests, new_len, chans)

    head_decay_values = jnp.exp(decay_rate)
    cum_new = jnp.cumsum(-(step_size * head_decay_values), axis=1)
    scaled = head_x.astype(jnp.float32).reshape(requests, new_len, heads_dev, head_dim)
    scaled = (scaled * step_size[..., None]).astype(jnp.bfloat16)

    positions = jnp.arange(cache_len, dtype=jnp.int32)
    token_order = jnp.arange(new_len, dtype=jnp.int32)
    live = positions[None, :] < lengths[:, None]
    masked = jnp.where(live[:, None, :], decay_cache, 0.0)
    local_sum = jnp.cumsum(masked, axis=2)
    tail_sum = local_sum[:, :, -1:] - local_sum

    col_scale = jnp.exp(tail_sum)
    row_scale = jnp.exp(cum_new)
    x_scaled = x_cache.astype(jnp.float32).reshape(requests, cache_len, heads_dev, head_dim)
    x_scaled = x_scaled * col_scale.transpose(0, 2, 1)[..., None]
    x_scaled = x_scaled.reshape(requests, cache_len, chans)
    x_hi = x_scaled.astype(jnp.bfloat16)
    x_lo = (x_scaled - x_hi.astype(jnp.float32)).astype(jnp.bfloat16)
    x_pair = jnp.concatenate([x_hi, x_lo], axis=-1)

    query_pos = lengths[:, None] + token_order[None, :]
    in_window = (query_pos[:, :, None] - positions[None, None, :] < windows[:, None, None]) & live[
        :, None, :
    ]
    score_old = jnp.einsum("rnk,rsk->rns", c_now, shared_b, preferred_element_type=jnp.float32)
    probs_old = jnp.where(in_window, score_old, 0.0).astype(jnp.bfloat16)
    acc = jnp.einsum("rns,rsc->rnc", probs_old, x_pair, preferred_element_type=jnp.float32)
    old_out = (acc[..., :chans] + acc[..., chans:]).reshape(requests, new_len, heads_dev, head_dim)
    old_out = old_out * row_scale[..., None]

    sink_b = jnp.take_along_axis(shared_b, sink_pos[:, :, None], axis=1)
    sink_x = jnp.take_along_axis(x_cache, sink_pos[:, :, None], axis=1)
    sink_live = sink_pos < lengths[:, None]
    sink_gap = query_pos[:, :, None] - sink_pos[:, None, :]
    sink_only = sink_live[:, None, :] & jnp.logical_not(sink_gap < windows[:, None, None])
    score_sink = jnp.einsum("rnk,rjk->rnj", c_now, sink_b, preferred_element_type=jnp.float32)
    probs_sink = jnp.where(sink_only, score_sink, 0.0).astype(jnp.bfloat16)
    sink_out = jnp.einsum("rnj,rjc->rnc", probs_sink, sink_x, preferred_element_type=jnp.float32)

    score_new = jnp.einsum("rnk,rjk->rnj", c_now, b_new, preferred_element_type=jnp.float32)
    new_gap = token_order[:, None] - token_order[None, :]
    keep_new = (new_gap[None] >= 0) & (new_gap[None] < windows[:, None, None])
    cum_t = cum_new.transpose(0, 2, 1)
    decay_new = jnp.exp(jnp.minimum(cum_t[:, :, :, None] - cum_t[:, :, None, :], 0.0))
    weight_new = jnp.where(keep_new[:, None], decay_new, 0.0)
    probs_new = (score_new[:, None] * weight_new).astype(jnp.bfloat16)
    new_out = jnp.einsum("rhnj,rjhd->rnhd", probs_new, scaled, preferred_element_type=jnp.float32)

    mixer_out = (old_out + new_out).reshape(requests, new_len, chans) + sink_out
    mixer_out = mixer_out.astype(jnp.bfloat16)

    back = mixer_out.reshape(requests, n_dev, tok_blk, chans).transpose(1, 0, 2, 3)
    back = lax.all_to_all(back, ("tz", "txc", "mlp"), 0, 0, tiled=True)
    back = back.reshape(n_tok, n_mlp, requests, tok_blk, chans).transpose(1, 2, 3, 0, 4)
    mixer_tok = lax.optimization_barrier(back.reshape(n_mlp * requests, tok_blk, n_tok * chans))

    gated_out = mixer_tok.astype(jnp.float32) * jax.nn.silu(gate_input.astype(jnp.float32))
    grouped = gated_out.reshape(gated_out.shape[0], gated_out.shape[1], groups, -1)
    norm_scale = lax.rsqrt(jnp.mean(grouped * grouped, axis=-1, keepdims=True) + EPS)
    normed = (grouped * norm_scale).reshape(gated_out.shape) * norm_gain
    return normed.astype(jnp.bfloat16)


def solution(mesh):
    n_tok, n_mlp = mesh.shape["tok"], mesh.shape["mlp"]
    split = Mesh(mesh.devices.reshape(GROUPS, n_tok // GROUPS, n_mlp), ("tz", "txc", "mlp"))
    tok = ("tz", "txc")
    return jax.shard_map(
        per_device,
        mesh=split,
        in_specs=(
            P(None, (*tok, "mlp"), None),
            P(None, (*tok, "mlp"), None),
            P(None, (*tok, "mlp"), None, None),
            P("mlp", None, tok),
            P(tok),
            P("mlp", None, tok),
            P("mlp", None, tok, None),
            P("mlp", tok, None),
            P("mlp"),
            P("mlp", None),
            P("mlp"),
            P(),
        ),
        out_specs=P(None, (*tok, "mlp"), None),
        check_vma=False,
    )
```

```python
import jax
import jax.numpy as jnp
from jax import lax
from jax.sharding import Mesh, PartitionSpec as P

EPS = 1e-05
GROUPS = 8


def mix_requests(
    head_x, b_new, c_now, shared_b, step_size, head_decay_values, x_cache, decay_cache,
    lengths, sink_pos, windows,
):
    requests, new_len, heads_dev = step_size.shape
    cache_len, chans = x_cache.shape[1], x_cache.shape[2]
    head_dim = chans // heads_dev
    cum_new = jnp.cumsum(-(step_size * head_decay_values), axis=1)
    scaled = head_x.astype(jnp.float32).reshape(requests, new_len, heads_dev, head_dim)
    scaled = (scaled * step_size[..., None]).astype(jnp.bfloat16)

    positions = jnp.arange(cache_len, dtype=jnp.int32)
    token_order = jnp.arange(new_len, dtype=jnp.int32)
    live = positions[None, :] < lengths[:, None]
    masked = jnp.where(live[:, None, :], decay_cache, 0.0)
    local_sum = jnp.cumsum(masked, axis=2)
    tail_sum = local_sum[:, :, -1:] - local_sum

    col_scale = jnp.exp(tail_sum)
    row_scale = jnp.exp(cum_new)
    x_scaled = x_cache.astype(jnp.float32).reshape(requests, cache_len, heads_dev, head_dim)
    x_scaled = x_scaled * col_scale.transpose(0, 2, 1)[..., None]
    x_scaled = x_scaled.reshape(requests, cache_len, chans)
    x_hi = x_scaled.astype(jnp.bfloat16)
    x_lo = (x_scaled - x_hi.astype(jnp.float32)).astype(jnp.bfloat16)
    x_pair = jnp.concatenate([x_hi, x_lo], axis=-1)

    query_pos = lengths[:, None] + token_order[None, :]
    in_window = (query_pos[:, :, None] - positions[None, None, :] < windows[:, None, None]) & live[
        :, None, :
    ]
    score_old = jnp.einsum("rnk,rsk->rns", c_now, shared_b, preferred_element_type=jnp.float32)
    probs_old = jnp.where(in_window, score_old, 0.0).astype(jnp.bfloat16)
    acc = jnp.einsum("rns,rsc->rnc", probs_old, x_pair, preferred_element_type=jnp.float32)
    old_out = (acc[..., :chans] + acc[..., chans:]).reshape(requests, new_len, heads_dev, head_dim)
    old_out = old_out * row_scale[..., None]

    sink_b = jnp.take_along_axis(shared_b, sink_pos[:, :, None], axis=1)
    sink_x = jnp.take_along_axis(x_cache, sink_pos[:, :, None], axis=1)
    sink_live = sink_pos < lengths[:, None]
    sink_gap = query_pos[:, :, None] - sink_pos[:, None, :]
    sink_only = sink_live[:, None, :] & jnp.logical_not(sink_gap < windows[:, None, None])
    score_sink = jnp.einsum("rnk,rjk->rnj", c_now, sink_b, preferred_element_type=jnp.float32)
    probs_sink = jnp.where(sink_only, score_sink, 0.0).astype(jnp.bfloat16)
    sink_out = jnp.einsum("rnj,rjc->rnc", probs_sink, sink_x, preferred_element_type=jnp.float32)

    score_new = jnp.einsum("rnk,rjk->rnj", c_now, b_new, preferred_element_type=jnp.float32)
    new_gap = token_order[:, None] - token_order[None, :]
    keep_new = (new_gap[None] >= 0) & (new_gap[None] < windows[:, None, None])
    cum_t = cum_new.transpose(0, 2, 1)
    decay_new = jnp.exp(jnp.minimum(cum_t[:, :, :, None] - cum_t[:, :, None, :], 0.0))
    weight_new = jnp.where(keep_new[:, None], decay_new, 0.0)
    probs_new = (score_new[:, None] * weight_new).astype(jnp.bfloat16)
    new_out = jnp.einsum("rhnj,rjhd->rnhd", probs_new, scaled, preferred_element_type=jnp.float32)

    mixer_out = (old_out + new_out).reshape(requests, new_len, chans) + sink_out
    mixer_out = mixer_out.astype(jnp.bfloat16)

    return mixer_out


def per_device(
    new_x,
    gate_input,
    state_proj,
    step_size,
    decay_rate,
    x_cache,
    b_cache,
    decay_cache,
    lengths,
    sink_pos,
    windows,
    norm_gain,
):
    n_tz = lax.axis_size("tz")
    n_txc = lax.axis_size("txc")
    n_tok = n_tz * n_txc
    n_mlp = lax.axis_size("mlp")
    n_dev = n_tok * n_mlp
    groups = state_proj.shape[2]
    state_dim = b_cache.shape[3]
    heads_dev = decay_rate.shape[0]
    requests = step_size.shape[0]
    new_len = step_size.shape[1]
    tok_blk = new_x.shape[1]
    cache_len = x_cache.shape[1]
    chans = x_cache.shape[2]
    head_dim = chans // heads_dev

    part_b = lax.all_to_all(b_cache, "tz", split_axis=1, concat_axis=1, tiled=True)
    sp = state_proj.reshape(n_mlp, requests, tok_blk, groups, 2 * state_dim)
    sp = sp.transpose(3, 0, 1, 2, 4).reshape(groups * n_mlp, requests, tok_blk, -1)
    sp = lax.all_to_all(sp, ("tz", "mlp"), 0, 0, tiled=True)
    sp = sp.reshape(n_tz, n_mlp, requests, tok_blk, -1).transpose(2, 0, 1, 3, 4)
    b_size = part_b.size // (requests * n_tz)
    packed = jnp.concatenate(
        [part_b.reshape(requests, n_tz, -1), sp.reshape(requests, n_tz, -1)], axis=2
    )
    packed = lax.all_gather(packed, "txc", axis=2)
    shared_b = packed[..., :b_size].reshape(requests, cache_len, state_dim)
    sp = packed[..., b_size:].reshape(requests, n_tz, n_txc, n_mlp, tok_blk, -1)
    sp = sp.reshape(requests, new_len, -1)
    b_new = sp[..., :state_dim]
    c_now = sp[..., state_dim:]

    x_part = new_x.reshape(n_mlp, requests, tok_blk, n_tok, chans).transpose(3, 0, 1, 2, 4)
    x_part = x_part.reshape(n_dev, requests, tok_blk, chans)
    head_x = lax.all_to_all(x_part, ("tz", "txc", "mlp"), 0, 0, tiled=True)
    head_x = head_x.transpose(1, 0, 2, 3).reshape(requests, new_len, chans)

    head_decay_values = jnp.exp(decay_rate)
    halves = 2
    half = requests // halves
    pieces = []
    for lo in range(0, requests, half):
        part = slice(lo, lo + half)
        mixed = mix_requests(
            head_x[part], b_new[part], c_now[part], shared_b[part], step_size[part],
            head_decay_values, x_cache[part], decay_cache[part], lengths[part],
            sink_pos[part], windows[part],
        )
        back = mixed.reshape(half, n_dev, tok_blk, chans).transpose(1, 0, 2, 3)
        back = lax.all_to_all(back, ("tz", "txc", "mlp"), 0, 0, tiled=True)
        pieces.append(back.reshape(n_tok, n_mlp, half, tok_blk, chans))
    back = jnp.stack(pieces, axis=2).transpose(1, 2, 3, 4, 0, 5)
    mixer_tok = lax.optimization_barrier(back.reshape(n_mlp * requests, tok_blk, n_tok * chans))

    gated_out = mixer_tok.astype(jnp.float32) * jax.nn.silu(gate_input.astype(jnp.float32))
    grouped = gated_out.reshape(gated_out.shape[0], gated_out.shape[1], groups, -1)
    norm_scale = lax.rsqrt(jnp.mean(grouped * grouped, axis=-1, keepdims=True) + EPS)
    normed = (grouped * norm_scale).reshape(gated_out.shape) * norm_gain
    return normed.astype(jnp.bfloat16)


def solution(mesh):
    n_tok, n_mlp = mesh.shape["tok"], mesh.shape["mlp"]
    split = Mesh(mesh.devices.reshape(GROUPS, n_tok // GROUPS, n_mlp), ("tz", "txc", "mlp"))
    tok = ("tz", "txc")
    return jax.shard_map(
        per_device,
        mesh=split,
        in_specs=(
            P(None, (*tok, "mlp"), None),
            P(None, (*tok, "mlp"), None),
            P(None, (*tok, "mlp"), None, None),
            P("mlp", None, tok),
            P(tok),
            P("mlp", None, tok),
            P("mlp", None, tok, None),
            P("mlp", tok, None),
            P("mlp"),
            P("mlp", None),
            P("mlp"),
            P(),
        ),
        out_specs=P(None, (*tok, "mlp"), None),
        check_vma=False,
    )
```

```python
import jax
import jax.numpy as jnp
from jax import lax
from jax.sharding import Mesh, PartitionSpec as P

EPS = 1e-05
GROUPS = 8


def per_device(
    new_x,
    gate_input,
    state_proj,
    step_size,
    decay_rate,
    x_cache,
    b_cache,
    decay_cache,
    lengths,
    sink_pos,
    windows,
    norm_gain,
):
    n_tz = lax.axis_size("tz")
    n_txc = lax.axis_size("txc")
    n_tok = n_tz * n_txc
    n_mlp = lax.axis_size("mlp")
    n_dev = n_tok * n_mlp
    groups = state_proj.shape[2]
    state_dim = b_cache.shape[3]
    heads_dev = decay_rate.shape[0]
    requests = step_size.shape[0]
    new_len = step_size.shape[1]
    tok_blk = new_x.shape[1]
    cache_len = x_cache.shape[1]
    chans = x_cache.shape[2]
    head_dim = chans // heads_dev

    x_part = new_x.reshape(n_mlp, requests, tok_blk, n_tok, chans).transpose(3, 0, 1, 2, 4)
    sp = state_proj.reshape(n_mlp, requests, tok_blk, groups, n_txc, -1)
    sp = sp.transpose(3, 4, 0, 1, 2, 5).reshape(n_tok, n_mlp, requests, tok_blk, -1)
    packed = jnp.concatenate([x_part, sp], axis=-1).reshape(n_dev, requests, tok_blk, -1)
    got = lax.all_to_all(packed, ("tz", "txc", "mlp"), 0, 0, tiled=True)
    got = got.transpose(1, 0, 2, 3).reshape(requests, new_len, -1)
    sp = lax.all_gather(got[..., chans:], "txc", axis=2).reshape(requests, new_len, -1)
    head_x = got[..., :chans]
    b_new = sp[..., :state_dim]
    c_now = sp[..., state_dim:]

    got, b_cache = lax.optimization_barrier((got, b_cache))
    part_b = lax.all_to_all(b_cache, "tz", split_axis=1, concat_axis=1, tiled=True)
    shared_b = lax.all_gather(part_b, "txc", axis=2)
    shared_b = shared_b.reshape(requests, cache_len, state_dim)

    head_decay_values = jnp.exp(decay_rate)
    cum_new = jnp.cumsum(-(step_size * head_decay_values), axis=1)
    scaled = head_x.astype(jnp.float32).reshape(requests, new_len, heads_dev, head_dim)
    scaled = (scaled * step_size[..., None]).astype(jnp.bfloat16)

    positions = jnp.arange(cache_len, dtype=jnp.int32)
    token_order = jnp.arange(new_len, dtype=jnp.int32)
    live = positions[None, :] < lengths[:, None]
    masked = jnp.where(live[:, None, :], decay_cache, 0.0)
    local_sum = jnp.cumsum(masked, axis=2)
    tail_sum = local_sum[:, :, -1:] - local_sum

    col_scale = jnp.exp(tail_sum)
    row_scale = jnp.exp(cum_new)
    x_scaled = x_cache.astype(jnp.float32).reshape(requests, cache_len, heads_dev, head_dim)
    x_scaled = x_scaled * col_scale.transpose(0, 2, 1)[..., None]
    x_scaled = x_scaled.reshape(requests, cache_len, chans)
    x_hi = x_scaled.astype(jnp.bfloat16)
    x_lo = (x_scaled - x_hi.astype(jnp.float32)).astype(jnp.bfloat16)
    x_pair = jnp.concatenate([x_hi, x_lo], axis=-1)

    query_pos = lengths[:, None] + token_order[None, :]
    in_window = (query_pos[:, :, None] - positions[None, None, :] < windows[:, None, None]) & live[
        :, None, :
    ]
    score_old = jnp.einsum("rnk,rsk->rns", c_now, shared_b, preferred_element_type=jnp.float32)
    probs_old = jnp.where(in_window, score_old, 0.0).astype(jnp.bfloat16)
    acc = jnp.einsum("rns,rsc->rnc", probs_old, x_pair, preferred_element_type=jnp.float32)
    old_out = (acc[..., :chans] + acc[..., chans:]).reshape(requests, new_len, heads_dev, head_dim)
    old_out = old_out * row_scale[..., None]

    sink_b = jnp.take_along_axis(shared_b, sink_pos[:, :, None], axis=1)
    sink_x = jnp.take_along_axis(x_cache, sink_pos[:, :, None], axis=1)
    sink_live = sink_pos < lengths[:, None]
    sink_gap = query_pos[:, :, None] - sink_pos[:, None, :]
    sink_only = sink_live[:, None, :] & jnp.logical_not(sink_gap < windows[:, None, None])
    score_sink = jnp.einsum("rnk,rjk->rnj", c_now, sink_b, preferred_element_type=jnp.float32)
    probs_sink = jnp.where(sink_only, score_sink, 0.0).astype(jnp.bfloat16)
    sink_out = jnp.einsum("rnj,rjc->rnc", probs_sink, sink_x, preferred_element_type=jnp.float32)

    score_new = jnp.einsum("rnk,rjk->rnj", c_now, b_new, preferred_element_type=jnp.float32)
    new_gap = token_order[:, None] - token_order[None, :]
    keep_new = (new_gap[None] >= 0) & (new_gap[None] < windows[:, None, None])
    cum_t = cum_new.transpose(0, 2, 1)
    decay_new = jnp.exp(jnp.minimum(cum_t[:, :, :, None] - cum_t[:, :, None, :], 0.0))
    weight_new = jnp.where(keep_new[:, None], decay_new, 0.0)
    probs_new = (score_new[:, None] * weight_new).astype(jnp.bfloat16)
    new_out = jnp.einsum("rhnj,rjhd->rnhd", probs_new, scaled, preferred_element_type=jnp.float32)

    mixer_out = (old_out + new_out).reshape(requests, new_len, chans) + sink_out
    mixer_out = mixer_out.astype(jnp.bfloat16)

    back = mixer_out.reshape(requests, n_dev, tok_blk, chans).transpose(1, 0, 2, 3)
    back = lax.all_to_all(back, ("tz", "txc", "mlp"), 0, 0, tiled=True)
    back = back.reshape(n_tok, n_mlp, requests, tok_blk, chans).transpose(1, 2, 3, 0, 4)
    mixer_tok = lax.optimization_barrier(back.reshape(n_mlp * requests, tok_blk, n_tok * chans))

    gated_out = mixer_tok.astype(jnp.float32) * jax.nn.silu(gate_input.astype(jnp.float32))
    grouped = gated_out.reshape(gated_out.shape[0], gated_out.shape[1], groups, -1)
    norm_scale = lax.rsqrt(jnp.mean(grouped * grouped, axis=-1, keepdims=True) + EPS)
    normed = (grouped * norm_scale).reshape(gated_out.shape) * norm_gain
    return normed.astype(jnp.bfloat16)


def solution(mesh):
    n_tok, n_mlp = mesh.shape["tok"], mesh.shape["mlp"]
    split = Mesh(mesh.devices.reshape(GROUPS, n_tok // GROUPS, n_mlp), ("tz", "txc", "mlp"))
    tok = ("tz", "txc")
    return jax.shard_map(
        per_device,
        mesh=split,
        in_specs=(
            P(None, (*tok, "mlp"), None),
            P(None, (*tok, "mlp"), None),
            P(None, (*tok, "mlp"), None, None),
            P("mlp", None, tok),
            P(tok),
            P("mlp", None, tok),
            P("mlp", None, tok, None),
            P("mlp", tok, None),
            P("mlp"),
            P("mlp", None),
            P("mlp"),
            P(),
        ),
        out_specs=P(None, (*tok, "mlp"), None),
        check_vma=False,
    )
```

```python
import jax
import jax.numpy as jnp
from jax import lax
from jax.sharding import Mesh, PartitionSpec as P

EPS = 1e-05
GROUPS = 8


def per_device(
    new_x,
    gate_input,
    state_proj,
    step_size,
    decay_rate,
    x_cache,
    b_cache,
    decay_cache,
    lengths,
    sink_pos,
    windows,
    norm_gain,
):
    n_tz = lax.axis_size("tz")
    n_txc = lax.axis_size("txc")
    n_tok = n_tz * n_txc
    n_mlp = lax.axis_size("mlp")
    n_dev = n_tok * n_mlp
    groups = state_proj.shape[2]
    state_dim = b_cache.shape[3]
    heads_dev = decay_rate.shape[0]
    requests = step_size.shape[0]
    new_len = step_size.shape[1]
    tok_blk = new_x.shape[1]
    cache_len = x_cache.shape[1]
    chans = x_cache.shape[2]
    head_dim = chans // heads_dev

    part_b = lax.all_to_all(b_cache, "tz", split_axis=1, concat_axis=1, tiled=True)
    shared_b = lax.all_gather(part_b, "txc", axis=2)
    shared_b = shared_b.reshape(requests, cache_len, state_dim)

    sp = state_proj.reshape(n_mlp, requests, tok_blk, groups, 2 * state_dim)
    sp = sp.transpose(3, 0, 1, 2, 4).reshape(groups * n_mlp, requests, tok_blk, -1)
    sp = lax.all_to_all(sp, ("tz", "mlp"), 0, 0, tiled=True)
    sp = lax.all_gather(sp, "txc", axis=1)
    sp = sp.reshape(n_tz, n_mlp, n_txc, requests, tok_blk, -1).transpose(3, 0, 2, 1, 4, 5)
    sp = sp.reshape(requests, new_len, -1)
    b_new = sp[..., :state_dim]
    c_now = sp[..., state_dim:]

    x_part = new_x.reshape(n_mlp, requests, tok_blk, n_tok, chans).transpose(3, 0, 1, 2, 4)
    x_part = x_part.reshape(n_dev, requests, tok_blk, chans)
    head_x = lax.all_to_all(x_part, ("tz", "txc", "mlp"), 0, 0, tiled=True)
    head_x = head_x.transpose(1, 0, 2, 3).reshape(requests, new_len, chans)

    head_decay_values = jnp.exp(decay_rate)
    cum_new = jnp.cumsum(-(step_size * head_decay_values), axis=1)
    scaled = head_x.astype(jnp.float32).reshape(requests, new_len, heads_dev, head_dim)
    scaled = (scaled * step_size[..., None]).astype(jnp.bfloat16)

    positions = jnp.arange(cache_len, dtype=jnp.int32)
    token_order = jnp.arange(new_len, dtype=jnp.int32)
    live = positions[None, :] < lengths[:, None]
    masked = jnp.where(live[:, None, :], decay_cache, 0.0)
    local_sum = jnp.cumsum(masked, axis=2)
    tail_sum = local_sum[:, :, -1:] - local_sum

    col_scale = jnp.exp(tail_sum)
    row_scale = jnp.exp(cum_new)
    x_scaled = x_cache.astype(jnp.float32).reshape(requests, cache_len, heads_dev, head_dim)
    x_scaled = x_scaled * col_scale.transpose(0, 2, 1)[..., None]
    x_scaled = x_scaled.reshape(requests, cache_len, chans)
    x_hi = x_scaled.astype(jnp.bfloat16)
    x_lo = (x_scaled - x_hi.astype(jnp.float32)).astype(jnp.bfloat16)
    x_pair = jnp.concatenate([x_hi, x_lo], axis=-1)

    query_pos = lengths[:, None] + token_order[None, :]
    score_new = jnp.einsum("rnk,rjk->rnj", c_now, b_new, preferred_element_type=jnp.float32)
    new_gap = token_order[:, None] - token_order[None, :]
    keep_new = (new_gap[None] >= 0) & (new_gap[None] < windows[:, None, None])
    cum_t = cum_new.transpose(0, 2, 1)
    decay_new = jnp.exp(jnp.minimum(cum_t[:, :, :, None] - cum_t[:, :, None, :], 0.0))
    weight_new = jnp.where(keep_new[:, None], decay_new, 0.0)
    probs_new = (score_new[:, None] * weight_new).astype(jnp.bfloat16)
    new_out = jnp.einsum("rhnj,rjhd->rnhd", probs_new, scaled, preferred_element_type=jnp.float32)


    new_out, x_pair, shared_b = lax.optimization_barrier((new_out, x_pair, shared_b))

    in_window = (query_pos[:, :, None] - positions[None, None, :] < windows[:, None, None]) & live[
        :, None, :
    ]
    score_old = jnp.einsum("rnk,rsk->rns", c_now, shared_b, preferred_element_type=jnp.float32)
    probs_old = jnp.where(in_window, score_old, 0.0).astype(jnp.bfloat16)
    acc = jnp.einsum("rns,rsc->rnc", probs_old, x_pair, preferred_element_type=jnp.float32)
    old_out = (acc[..., :chans] + acc[..., chans:]).reshape(requests, new_len, heads_dev, head_dim)
    old_out = old_out * row_scale[..., None]

    sink_b = jnp.take_along_axis(shared_b, sink_pos[:, :, None], axis=1)
    sink_x = jnp.take_along_axis(x_cache, sink_pos[:, :, None], axis=1)
    sink_live = sink_pos < lengths[:, None]
    sink_gap = query_pos[:, :, None] - sink_pos[:, None, :]
    sink_only = sink_live[:, None, :] & jnp.logical_not(sink_gap < windows[:, None, None])
    score_sink = jnp.einsum("rnk,rjk->rnj", c_now, sink_b, preferred_element_type=jnp.float32)
    probs_sink = jnp.where(sink_only, score_sink, 0.0).astype(jnp.bfloat16)
    sink_out = jnp.einsum("rnj,rjc->rnc", probs_sink, sink_x, preferred_element_type=jnp.float32)

    mixer_out = (old_out + new_out).reshape(requests, new_len, chans) + sink_out
    mixer_out = mixer_out.astype(jnp.bfloat16)

    back = mixer_out.reshape(requests, n_dev, tok_blk, chans).transpose(1, 0, 2, 3)
    back = lax.all_to_all(back, ("tz", "txc", "mlp"), 0, 0, tiled=True)
    back = back.reshape(n_tok, n_mlp, requests, tok_blk, chans).transpose(1, 2, 3, 0, 4)
    mixer_tok = lax.optimization_barrier(back.reshape(n_mlp * requests, tok_blk, n_tok * chans))

    gated_out = mixer_tok.astype(jnp.float32) * jax.nn.silu(gate_input.astype(jnp.float32))
    grouped = gated_out.reshape(gated_out.shape[0], gated_out.shape[1], groups, -1)
    norm_scale = lax.rsqrt(jnp.mean(grouped * grouped, axis=-1, keepdims=True) + EPS)
    normed = (grouped * norm_scale).reshape(gated_out.shape) * norm_gain
    return normed.astype(jnp.bfloat16)


def solution(mesh):
    n_tok, n_mlp = mesh.shape["tok"], mesh.shape["mlp"]
    split = Mesh(mesh.devices.reshape(GROUPS, n_tok // GROUPS, n_mlp), ("tz", "txc", "mlp"))
    tok = ("tz", "txc")
    return jax.shard_map(
        per_device,
        mesh=split,
        in_specs=(
            P(None, (*tok, "mlp"), None),
            P(None, (*tok, "mlp"), None),
            P(None, (*tok, "mlp"), None, None),
            P("mlp", None, tok),
            P(tok),
            P("mlp", None, tok),
            P("mlp", None, tok, None),
            P("mlp", tok, None),
            P("mlp"),
            P("mlp", None),
            P("mlp"),
            P(),
        ),
        out_specs=P(None, (*tok, "mlp"), None),
        check_vma=False,
    )
```

```python
import jax
import jax.numpy as jnp
from jax import lax
from jax.sharding import Mesh, PartitionSpec as P

EPS = 1e-05
GROUPS = 8


def per_device(
    new_x,
    gate_input,
    state_proj,
    step_size,
    decay_rate,
    x_cache,
    b_cache,
    decay_cache,
    lengths,
    sink_pos,
    windows,
    norm_gain,
):
    n_tz = lax.axis_size("tz")
    n_txc = lax.axis_size("txc")
    n_tok = n_tz * n_txc
    n_mlp = lax.axis_size("mlp")
    n_dev = n_tok * n_mlp
    groups = state_proj.shape[2]
    state_dim = b_cache.shape[3]
    heads_dev = decay_rate.shape[0]
    requests = step_size.shape[0]
    new_len = step_size.shape[1]
    tok_blk = new_x.shape[1]
    cache_len = x_cache.shape[1]
    chans = x_cache.shape[2]
    head_dim = chans // heads_dev

    part_b = lax.all_to_all(b_cache, "tz", split_axis=1, concat_axis=1, tiled=True)
    shared_b = lax.all_gather(part_b, "txc", axis=2)
    shared_b = shared_b.reshape(requests, cache_len, state_dim)

    sp = state_proj.reshape(n_mlp, requests, tok_blk, groups, 2 * state_dim)
    sp = sp.transpose(3, 0, 1, 2, 4).reshape(groups * n_mlp, requests, tok_blk, -1)
    sp = lax.all_to_all(sp, ("tz", "mlp"), 0, 0, tiled=True)
    sp = lax.all_gather(sp, "txc", axis=1)
    sp = sp.reshape(n_tz, n_mlp, n_txc, requests, tok_blk, -1).transpose(3, 0, 2, 1, 4, 5)
    sp = sp.reshape(requests, new_len, -1)
    b_new = sp[..., :state_dim]
    c_now = sp[..., state_dim:]

    x_part = new_x.reshape(n_mlp, requests, tok_blk, n_tok, chans).transpose(3, 0, 1, 2, 4)
    x_part = x_part.reshape(n_dev, requests, tok_blk, chans)
    head_x = lax.all_to_all(x_part, ("tz", "txc", "mlp"), 0, 0, tiled=True)
    head_x = head_x.transpose(1, 0, 2, 3).reshape(requests, new_len, chans)

    head_decay_values = jnp.exp(decay_rate)
    cum_new = jnp.cumsum(-(step_size * head_decay_values), axis=1)
    scaled = head_x.astype(jnp.float32).reshape(requests, new_len, heads_dev, head_dim)
    scaled = (scaled * step_size[..., None]).astype(jnp.bfloat16)

    positions = jnp.arange(cache_len, dtype=jnp.int32)
    token_order = jnp.arange(new_len, dtype=jnp.int32)
    live = positions[None, :] < lengths[:, None]
    masked = jnp.where(live[:, None, :], decay_cache, 0.0)
    local_sum = jnp.cumsum(masked, axis=2)
    tail_sum = local_sum[:, :, -1:] - local_sum

    col_scale = jnp.exp(tail_sum)
    row_scale = jnp.exp(cum_new)
    x_scaled = x_cache.astype(jnp.float32).reshape(requests, cache_len, heads_dev, head_dim)
    x_scaled = x_scaled * col_scale.transpose(0, 2, 1)[..., None]
    x_scaled = x_scaled.reshape(requests, cache_len, chans)
    x_pair = x_scaled.astype(jnp.bfloat16)

    query_pos = lengths[:, None] + token_order[None, :]
    score_new = jnp.einsum("rnk,rjk->rnj", c_now, b_new, preferred_element_type=jnp.float32)
    new_gap = token_order[:, None] - token_order[None, :]
    keep_new = (new_gap[None] >= 0) & (new_gap[None] < windows[:, None, None])
    cum_t = cum_new.transpose(0, 2, 1)
    decay_new = jnp.exp(jnp.minimum(cum_t[:, :, :, None] - cum_t[:, :, None, :], 0.0))
    weight_new = jnp.where(keep_new[:, None], decay_new, 0.0)
    probs_new = (score_new[:, None] * weight_new).astype(jnp.bfloat16)
    new_out = jnp.einsum("rhnj,rjhd->rnhd", probs_new, scaled, preferred_element_type=jnp.float32)


    new_out, x_pair, shared_b = lax.optimization_barrier((new_out, x_pair, shared_b))

    in_window = (query_pos[:, :, None] - positions[None, None, :] < windows[:, None, None]) & live[
        :, None, :
    ]
    score_old = jnp.einsum("rnk,rsk->rns", c_now, shared_b, preferred_element_type=jnp.float32)
    probs_old = jnp.where(in_window, score_old, 0.0).astype(jnp.bfloat16)
    acc = jnp.einsum("rns,rsc->rnc", probs_old, x_pair, preferred_element_type=jnp.float32)
    old_out = acc.reshape(requests, new_len, heads_dev, head_dim)
    old_out = old_out * row_scale[..., None]

    sink_b = jnp.take_along_axis(shared_b, sink_pos[:, :, None], axis=1)
    sink_x = jnp.take_along_axis(x_cache, sink_pos[:, :, None], axis=1)
    sink_live = sink_pos < lengths[:, None]
    sink_gap = query_pos[:, :, None] - sink_pos[:, None, :]
    sink_only = sink_live[:, None, :] & jnp.logical_not(sink_gap < windows[:, None, None])
    score_sink = jnp.einsum("rnk,rjk->rnj", c_now, sink_b, preferred_element_type=jnp.float32)
    probs_sink = jnp.where(sink_only, score_sink, 0.0).astype(jnp.bfloat16)
    sink_out = jnp.einsum("rnj,rjc->rnc", probs_sink, sink_x, preferred_element_type=jnp.float32)

    mixer_out = (old_out + new_out).reshape(requests, new_len, chans) + sink_out
    mixer_out = mixer_out.astype(jnp.bfloat16)

    back = mixer_out.reshape(requests, n_dev, tok_blk, chans).transpose(1, 0, 2, 3)
    back = lax.all_to_all(back, ("tz", "txc", "mlp"), 0, 0, tiled=True)
    back = back.reshape(n_tok, n_mlp, requests, tok_blk, chans).transpose(1, 2, 3, 0, 4)
    mixer_tok = lax.optimization_barrier(back.reshape(n_mlp * requests, tok_blk, n_tok * chans))

    gated_out = mixer_tok.astype(jnp.float32) * jax.nn.silu(gate_input.astype(jnp.float32))
    grouped = gated_out.reshape(gated_out.shape[0], gated_out.shape[1], groups, -1)
    norm_scale = lax.rsqrt(jnp.mean(grouped * grouped, axis=-1, keepdims=True) + EPS)
    normed = (grouped * norm_scale).reshape(gated_out.shape) * norm_gain
    return normed.astype(jnp.bfloat16)


def solution(mesh):
    n_tok, n_mlp = mesh.shape["tok"], mesh.shape["mlp"]
    split = Mesh(mesh.devices.reshape(GROUPS, n_tok // GROUPS, n_mlp), ("tz", "txc", "mlp"))
    tok = ("tz", "txc")
    return jax.shard_map(
        per_device,
        mesh=split,
        in_specs=(
            P(None, (*tok, "mlp"), None),
            P(None, (*tok, "mlp"), None),
            P(None, (*tok, "mlp"), None, None),
            P("mlp", None, tok),
            P(tok),
            P("mlp", None, tok),
            P("mlp", None, tok, None),
            P("mlp", tok, None),
            P("mlp"),
            P("mlp", None),
            P("mlp"),
            P(),
        ),
        out_specs=P(None, (*tok, "mlp"), None),
        check_vma=False,
    )
```

```python
import jax
import jax.numpy as jnp
from jax import lax
from jax.sharding import Mesh, PartitionSpec as P

EPS = 1e-05
GROUPS = 8


def per_device(
    new_x,
    gate_input,
    state_proj,
    step_size,
    decay_rate,
    x_cache,
    b_cache,
    decay_cache,
    lengths,
    sink_pos,
    windows,
    norm_gain,
):
    n_tz = lax.axis_size("tz")
    n_txc = lax.axis_size("txc")
    n_tok = n_tz * n_txc
    n_mlp = lax.axis_size("mlp")
    n_dev = n_tok * n_mlp
    groups = state_proj.shape[2]
    state_dim = b_cache.shape[3]
    heads_dev = decay_rate.shape[0]
    requests = step_size.shape[0]
    new_len = step_size.shape[1]
    tok_blk = new_x.shape[1]
    cache_len = x_cache.shape[1]
    chans = x_cache.shape[2]
    head_dim = chans // heads_dev

    part_b = lax.all_to_all(b_cache, "tz", split_axis=1, concat_axis=1, tiled=True)
    shared_b = lax.all_gather(part_b, "txc", axis=2)
    shared_b = shared_b.reshape(requests, n_tz, cache_len // n_tz, state_dim)

    sp = state_proj.reshape(n_mlp, requests, tok_blk, groups, 2 * state_dim)
    sp = sp.transpose(3, 0, 1, 2, 4).reshape(groups * n_mlp, requests, tok_blk, -1)
    sp = lax.all_to_all(sp, ("tz", "mlp"), 0, 0, tiled=True)
    sp = lax.all_gather(sp, "txc", axis=1)
    sp = sp.reshape(n_tz, n_mlp, n_txc, requests, tok_blk, -1).transpose(3, 0, 2, 1, 4, 5)
    sp = sp.reshape(requests, new_len, -1)
    b_new = sp[..., :state_dim]
    c_now = sp[..., state_dim:]

    x_part = new_x.reshape(n_mlp, requests, tok_blk, n_tok, chans).transpose(3, 0, 1, 2, 4)
    x_part = x_part.reshape(n_dev, requests, tok_blk, chans)
    head_x = lax.all_to_all(x_part, ("tz", "txc", "mlp"), 0, 0, tiled=True)
    head_x = head_x.transpose(1, 0, 2, 3).reshape(requests, new_len, chans)

    head_decay_values = jnp.exp(decay_rate)
    cum_new = jnp.cumsum(-(step_size * head_decay_values), axis=1)
    scaled = head_x.astype(jnp.float32).reshape(requests, new_len, heads_dev, head_dim)
    scaled = (scaled * step_size[..., None]).astype(jnp.bfloat16)

    positions = jnp.arange(cache_len, dtype=jnp.int32)
    token_order = jnp.arange(new_len, dtype=jnp.int32)
    live = positions[None, :] < lengths[:, None]
    masked = jnp.where(live[:, None, :], decay_cache, 0.0)
    local_sum = jnp.cumsum(masked, axis=2)
    tail_sum = local_sum[:, :, -1:] - local_sum

    col_scale = jnp.exp(tail_sum)
    row_scale = jnp.exp(cum_new)
    x_scaled = x_cache.astype(jnp.float32).reshape(requests, cache_len, heads_dev, head_dim)
    x_scaled = x_scaled * col_scale.transpose(0, 2, 1)[..., None]
    x_scaled = x_scaled.reshape(requests, cache_len, chans)
    x_pair = x_scaled.astype(jnp.bfloat16)

    query_pos = lengths[:, None] + token_order[None, :]
    score_new = jnp.einsum("rnk,rjk->rnj", c_now, b_new, preferred_element_type=jnp.float32)
    new_gap = token_order[:, None] - token_order[None, :]
    keep_new = (new_gap[None] >= 0) & (new_gap[None] < windows[:, None, None])
    cum_t = cum_new.transpose(0, 2, 1)
    decay_new = jnp.exp(jnp.minimum(cum_t[:, :, :, None] - cum_t[:, :, None, :], 0.0))
    weight_new = jnp.where(keep_new[:, None], decay_new, 0.0)
    probs_new = (score_new[:, None] * weight_new).astype(jnp.bfloat16)
    new_out = jnp.einsum("rhnj,rjhd->rnhd", probs_new, scaled, preferred_element_type=jnp.float32)


    new_out, x_pair, shared_b = lax.optimization_barrier((new_out, x_pair, shared_b))

    in_window = (query_pos[:, :, None] - positions[None, None, :] < windows[:, None, None]) & live[
        :, None, :
    ]
    score_old = jnp.einsum("rnk,rtqk->rntq", c_now, shared_b, preferred_element_type=jnp.float32)
    score_old = score_old.reshape(requests, new_len, cache_len)
    probs_old = jnp.where(in_window, score_old, 0.0).astype(jnp.bfloat16)
    acc = jnp.einsum("rns,rsc->rnc", probs_old, x_pair, preferred_element_type=jnp.float32)
    old_out = acc.reshape(requests, new_len, heads_dev, head_dim)
    old_out = old_out * row_scale[..., None]

    per_tz = cache_len // n_tz
    request_ids = jnp.arange(requests, dtype=jnp.int32)[:, None]
    sink_b = shared_b[request_ids, sink_pos // per_tz, sink_pos % per_tz]
    sink_x = jnp.take_along_axis(x_cache, sink_pos[:, :, None], axis=1)
    sink_live = sink_pos < lengths[:, None]
    sink_gap = query_pos[:, :, None] - sink_pos[:, None, :]
    sink_only = sink_live[:, None, :] & jnp.logical_not(sink_gap < windows[:, None, None])
    score_sink = jnp.einsum("rnk,rjk->rnj", c_now, sink_b, preferred_element_type=jnp.float32)
    probs_sink = jnp.where(sink_only, score_sink, 0.0).astype(jnp.bfloat16)
    sink_out = jnp.einsum("rnj,rjc->rnc", probs_sink, sink_x, preferred_element_type=jnp.float32)

    mixer_out = (old_out + new_out).reshape(requests, new_len, chans) + sink_out
    mixer_out = mixer_out.astype(jnp.bfloat16)

    back = mixer_out.reshape(requests, n_dev, tok_blk, chans).transpose(1, 0, 2, 3)
    back = lax.all_to_all(back, ("tz", "txc", "mlp"), 0, 0, tiled=True)
    back = back.reshape(n_tok, n_mlp, requests, tok_blk, chans).transpose(1, 2, 3, 0, 4)
    mixer_tok = lax.optimization_barrier(back.reshape(n_mlp * requests, tok_blk, n_tok * chans))

    gated_out = mixer_tok.astype(jnp.float32) * jax.nn.silu(gate_input.astype(jnp.float32))
    grouped = gated_out.reshape(gated_out.shape[0], gated_out.shape[1], groups, -1)
    norm_scale = lax.rsqrt(jnp.mean(grouped * grouped, axis=-1, keepdims=True) + EPS)
    normed = (grouped * norm_scale).reshape(gated_out.shape) * norm_gain
    return normed.astype(jnp.bfloat16)


def solution(mesh):
    n_tok, n_mlp = mesh.shape["tok"], mesh.shape["mlp"]
    split = Mesh(mesh.devices.reshape(GROUPS, n_tok // GROUPS, n_mlp), ("tz", "txc", "mlp"))
    tok = ("tz", "txc")
    return jax.shard_map(
        per_device,
        mesh=split,
        in_specs=(
            P(None, (*tok, "mlp"), None),
            P(None, (*tok, "mlp"), None),
            P(None, (*tok, "mlp"), None, None),
            P("mlp", None, tok),
            P(tok),
            P("mlp", None, tok),
            P("mlp", None, tok, None),
            P("mlp", tok, None),
            P("mlp"),
            P("mlp", None),
            P("mlp"),
            P(),
        ),
        out_specs=P(None, (*tok, "mlp"), None),
        check_vma=False,
    )
```

```python
import jax
import jax.numpy as jnp
from jax import lax
from jax.sharding import Mesh, PartitionSpec as P

EPS = 1e-05
GROUPS = 8
WINDOW_LIMIT = 2048


def per_device(
    new_x,
    gate_input,
    state_proj,
    step_size,
    decay_rate,
    x_cache,
    b_cache,
    decay_cache,
    lengths,
    sink_pos,
    windows,
    norm_gain,
):
    n_tz = lax.axis_size("tz")
    n_txc = lax.axis_size("txc")
    n_tok = n_tz * n_txc
    n_mlp = lax.axis_size("mlp")
    n_dev = n_tok * n_mlp
    groups = state_proj.shape[2]
    state_dim = b_cache.shape[3]
    heads_dev = decay_rate.shape[0]
    requests = step_size.shape[0]
    new_len = step_size.shape[1]
    tok_blk = new_x.shape[1]
    cache_len = x_cache.shape[1]
    chans = x_cache.shape[2]
    head_dim = chans // heads_dev

    part_b = lax.all_to_all(b_cache, "tz", split_axis=1, concat_axis=1, tiled=True)
    shared_b = lax.all_gather(part_b, "txc", axis=2)
    shared_b = shared_b.reshape(requests, cache_len, state_dim)

    sp = state_proj.reshape(n_mlp, requests, tok_blk, groups, 2 * state_dim)
    sp = sp.transpose(3, 0, 1, 2, 4).reshape(groups * n_mlp, requests, tok_blk, -1)
    sp = lax.all_to_all(sp, ("tz", "mlp"), 0, 0, tiled=True)
    sp = lax.all_gather(sp, "txc", axis=1)
    sp = sp.reshape(n_tz, n_mlp, n_txc, requests, tok_blk, -1).transpose(3, 0, 2, 1, 4, 5)
    sp = sp.reshape(requests, new_len, -1)
    b_new = sp[..., :state_dim]
    c_now = sp[..., state_dim:]

    x_part = new_x.reshape(n_mlp, requests, tok_blk, n_tok, chans).transpose(3, 0, 1, 2, 4)
    x_part = x_part.reshape(n_dev, requests, tok_blk, chans)
    head_x = lax.all_to_all(x_part, ("tz", "txc", "mlp"), 0, 0, tiled=True)
    head_x = head_x.transpose(1, 0, 2, 3).reshape(requests, new_len, chans)

    head_decay_values = jnp.exp(decay_rate)
    cum_new = jnp.cumsum(-(step_size * head_decay_values), axis=1)
    scaled = head_x.astype(jnp.float32).reshape(requests, new_len, heads_dev, head_dim)
    scaled = (scaled * step_size[..., None]).astype(jnp.bfloat16)

    positions = jnp.arange(cache_len, dtype=jnp.int32)
    token_order = jnp.arange(new_len, dtype=jnp.int32)
    live = positions[None, :] < lengths[:, None]
    masked = jnp.where(live[:, None, :], decay_cache, 0.0)
    local_sum = jnp.cumsum(masked, axis=2)
    tail_sum = local_sum[:, :, -1:] - local_sum

    col_scale = jnp.exp(tail_sum)
    row_scale = jnp.exp(cum_new)
    x_scaled = x_cache.astype(jnp.float32).reshape(requests, cache_len, heads_dev, head_dim)
    x_scaled = x_scaled * col_scale.transpose(0, 2, 1)[..., None]
    x_scaled = x_scaled.reshape(requests, cache_len, chans)
    x_pair = x_scaled.astype(jnp.bfloat16)

    query_pos = lengths[:, None] + token_order[None, :]
    score_new = jnp.einsum("rnk,rjk->rnj", c_now, b_new, preferred_element_type=jnp.float32)
    new_gap = token_order[:, None] - token_order[None, :]
    keep_new = (new_gap[None] >= 0) & (new_gap[None] < windows[:, None, None])
    cum_t = cum_new.transpose(0, 2, 1)
    decay_new = jnp.exp(jnp.minimum(cum_t[:, :, :, None] - cum_t[:, :, None, :], 0.0))
    weight_new = jnp.where(keep_new[:, None], decay_new, 0.0)
    probs_new = (score_new[:, None] * weight_new).astype(jnp.bfloat16)
    new_out = jnp.einsum("rhnj,rjhd->rnhd", probs_new, scaled, preferred_element_type=jnp.float32)


    new_out, x_pair, shared_b = lax.optimization_barrier((new_out, x_pair, shared_b))

    win = min(WINDOW_LIMIT, cache_len)
    start = jnp.clip(lengths - win, 0, cache_len - win)
    take = jax.vmap(lambda a, at: lax.dynamic_slice_in_dim(a, at, win, 0))
    b_win = take(shared_b, start)
    x_win = take(x_pair, start)
    pos_win = start[:, None] + jnp.arange(win, dtype=jnp.int32)[None, :]
    in_window = (query_pos[:, :, None] - pos_win[:, None, :] < windows[:, None, None]) & (
        pos_win < lengths[:, None]
    )[:, None, :]
    score_old = jnp.einsum("rnk,rsk->rns", c_now, b_win, preferred_element_type=jnp.float32)
    probs_old = jnp.where(in_window, score_old, 0.0).astype(jnp.bfloat16)
    acc = jnp.einsum("rns,rsc->rnc", probs_old, x_win, preferred_element_type=jnp.float32)
    old_out = acc.reshape(requests, new_len, heads_dev, head_dim)
    old_out = old_out * row_scale[..., None]

    sink_b = jnp.take_along_axis(shared_b, sink_pos[:, :, None], axis=1)
    sink_x = jnp.take_along_axis(x_cache, sink_pos[:, :, None], axis=1)
    sink_live = sink_pos < lengths[:, None]
    sink_gap = query_pos[:, :, None] - sink_pos[:, None, :]
    sink_only = sink_live[:, None, :] & jnp.logical_not(sink_gap < windows[:, None, None])
    score_sink = jnp.einsum("rnk,rjk->rnj", c_now, sink_b, preferred_element_type=jnp.float32)
    probs_sink = jnp.where(sink_only, score_sink, 0.0).astype(jnp.bfloat16)
    sink_out = jnp.einsum("rnj,rjc->rnc", probs_sink, sink_x, preferred_element_type=jnp.float32)

    mixer_out = (old_out + new_out).reshape(requests, new_len, chans) + sink_out
    mixer_out = mixer_out.astype(jnp.bfloat16)

    back = mixer_out.reshape(requests, n_dev, tok_blk, chans).transpose(1, 0, 2, 3)
    back = lax.all_to_all(back, ("tz", "txc", "mlp"), 0, 0, tiled=True)
    back = back.reshape(n_tok, n_mlp, requests, tok_blk, chans).transpose(1, 2, 3, 0, 4)
    mixer_tok = lax.optimization_barrier(back.reshape(n_mlp * requests, tok_blk, n_tok * chans))

    gated_out = mixer_tok.astype(jnp.float32) * jax.nn.silu(gate_input.astype(jnp.float32))
    grouped = gated_out.reshape(gated_out.shape[0], gated_out.shape[1], groups, -1)
    norm_scale = lax.rsqrt(jnp.mean(grouped * grouped, axis=-1, keepdims=True) + EPS)
    normed = (grouped * norm_scale).reshape(gated_out.shape) * norm_gain
    return normed.astype(jnp.bfloat16)


def solution(mesh):
    n_tok, n_mlp = mesh.shape["tok"], mesh.shape["mlp"]
    split = Mesh(mesh.devices.reshape(GROUPS, n_tok // GROUPS, n_mlp), ("tz", "txc", "mlp"))
    tok = ("tz", "txc")
    return jax.shard_map(
        per_device,
        mesh=split,
        in_specs=(
            P(None, (*tok, "mlp"), None),
            P(None, (*tok, "mlp"), None),
            P(None, (*tok, "mlp"), None, None),
            P("mlp", None, tok),
            P(tok),
            P("mlp", None, tok),
            P("mlp", None, tok, None),
            P("mlp", tok, None),
            P("mlp"),
            P("mlp", None),
            P("mlp"),
            P(),
        ),
        out_specs=P(None, (*tok, "mlp"), None),
        check_vma=False,
    )
```

```python
import jax
import jax.numpy as jnp
from jax import lax
from jax.sharding import Mesh, PartitionSpec as P

EPS = 1e-05
GROUPS = 8
WINDOW_LIMIT = 2048


def per_device(
    new_x,
    gate_input,
    state_proj,
    step_size,
    decay_rate,
    x_cache,
    b_cache,
    decay_cache,
    lengths,
    sink_pos,
    windows,
    norm_gain,
):
    n_tz = lax.axis_size("tz")
    n_txc = lax.axis_size("txc")
    n_tok = n_tz * n_txc
    n_mlp = lax.axis_size("mlp")
    n_dev = n_tok * n_mlp
    groups = state_proj.shape[2]
    state_dim = b_cache.shape[3]
    heads_dev = decay_rate.shape[0]
    requests = step_size.shape[0]
    new_len = step_size.shape[1]
    tok_blk = new_x.shape[1]
    cache_len = x_cache.shape[1]
    chans = x_cache.shape[2]
    head_dim = chans // heads_dev

    part_b = lax.all_to_all(b_cache, "tz", split_axis=1, concat_axis=1, tiled=True)
    shared_b = lax.all_gather(part_b, "txc", axis=2)
    shared_b = shared_b.reshape(requests, cache_len, state_dim)

    sp = state_proj.reshape(n_mlp, requests, tok_blk, groups, 2 * state_dim)
    sp = sp.transpose(3, 0, 1, 2, 4).reshape(groups * n_mlp, requests, tok_blk, -1)
    sp = lax.all_to_all(sp, ("tz", "mlp"), 0, 0, tiled=True)
    sp = lax.all_gather(sp, "txc", axis=1)
    sp = sp.reshape(n_tz, n_mlp, n_txc, requests, tok_blk, -1).transpose(3, 0, 2, 1, 4, 5)
    sp = sp.reshape(requests, new_len, -1)
    b_new = sp[..., :state_dim]
    c_now = sp[..., state_dim:]

    x_part = new_x.reshape(n_mlp, requests, tok_blk, n_tok, chans).transpose(3, 0, 1, 2, 4)
    x_part = x_part.reshape(n_dev, requests, tok_blk, chans)
    head_x = lax.all_to_all(x_part, ("tz", "txc", "mlp"), 0, 0, tiled=True)
    head_x = head_x.transpose(1, 0, 2, 3).reshape(requests, new_len, chans)

    head_decay_values = jnp.exp(decay_rate)
    cum_new = jnp.cumsum(-(step_size * head_decay_values), axis=1)
    scaled = head_x.astype(jnp.float32).reshape(requests, new_len, heads_dev, head_dim)
    scaled = (scaled * step_size[..., None]).astype(jnp.bfloat16)

    positions = jnp.arange(cache_len, dtype=jnp.int32)
    token_order = jnp.arange(new_len, dtype=jnp.int32)
    live = positions[None, :] < lengths[:, None]
    masked = jnp.where(live[:, None, :], decay_cache, 0.0)
    local_sum = jnp.cumsum(masked, axis=2)
    tail_sum = local_sum[:, :, -1:] - local_sum

    col_scale = jnp.exp(tail_sum)
    row_scale = jnp.exp(cum_new)
    x_scaled = x_cache.astype(jnp.float32).reshape(requests, cache_len, heads_dev, head_dim)
    x_scaled = x_scaled * col_scale.transpose(0, 2, 1)[..., None]
    x_scaled = x_scaled.reshape(requests, cache_len, chans)
    x_pair = x_scaled.astype(jnp.bfloat16)

    query_pos = lengths[:, None] + token_order[None, :]
    score_new = jnp.einsum("rnk,rjk->rnj", c_now, b_new, preferred_element_type=jnp.float32)
    new_gap = token_order[:, None] - token_order[None, :]
    keep_new = (new_gap[None] >= 0) & (new_gap[None] < windows[:, None, None])
    cum_t = cum_new.transpose(0, 2, 1)
    decay_new = jnp.exp(jnp.minimum(cum_t[:, :, :, None] - cum_t[:, :, None, :], 0.0))
    weight_new = jnp.where(keep_new[:, None], decay_new, 0.0)
    probs_new = (score_new[:, None] * weight_new).astype(jnp.bfloat16)
    new_out = jnp.einsum("rhnj,rjhd->rnhd", probs_new, scaled, preferred_element_type=jnp.float32)


    new_out, x_pair, shared_b = lax.optimization_barrier((new_out, x_pair, shared_b))

    win = min(WINDOW_LIMIT, cache_len)
    start = jnp.clip(lengths - win, 0, cache_len - win)
    pos_win = start[:, None] + jnp.arange(win, dtype=jnp.int32)[None, :]
    in_window = (query_pos[:, :, None] - pos_win[:, None, :] < windows[:, None, None]) & (
        pos_win < lengths[:, None]
    )[:, None, :]
    accs = []
    for r in range(requests):
        b_win = lax.dynamic_slice_in_dim(shared_b[r], start[r], win, 0)
        x_win = lax.dynamic_slice_in_dim(x_pair[r], start[r], win, 0)
        score_old = jnp.dot(c_now[r], b_win.T, preferred_element_type=jnp.float32)
        probs_old = jnp.where(in_window[r], score_old, 0.0).astype(jnp.bfloat16)
        accs.append(jnp.dot(probs_old, x_win, preferred_element_type=jnp.float32))
    acc = jnp.stack(accs)
    old_out = acc.reshape(requests, new_len, heads_dev, head_dim)
    old_out = old_out * row_scale[..., None]

    sink_b = jnp.take_along_axis(shared_b, sink_pos[:, :, None], axis=1)
    sink_x = jnp.take_along_axis(x_cache, sink_pos[:, :, None], axis=1)
    sink_live = sink_pos < lengths[:, None]
    sink_gap = query_pos[:, :, None] - sink_pos[:, None, :]
    sink_only = sink_live[:, None, :] & jnp.logical_not(sink_gap < windows[:, None, None])
    score_sink = jnp.einsum("rnk,rjk->rnj", c_now, sink_b, preferred_element_type=jnp.float32)
    probs_sink = jnp.where(sink_only, score_sink, 0.0).astype(jnp.bfloat16)
    sink_out = jnp.einsum("rnj,rjc->rnc", probs_sink, sink_x, preferred_element_type=jnp.float32)

    mixer_out = (old_out + new_out).reshape(requests, new_len, chans) + sink_out
    mixer_out = mixer_out.astype(jnp.bfloat16)

    back = mixer_out.reshape(requests, n_dev, tok_blk, chans).transpose(1, 0, 2, 3)
    back = lax.all_to_all(back, ("tz", "txc", "mlp"), 0, 0, tiled=True)
    back = back.reshape(n_tok, n_mlp, requests, tok_blk, chans).transpose(1, 2, 3, 0, 4)
    mixer_tok = lax.optimization_barrier(back.reshape(n_mlp * requests, tok_blk, n_tok * chans))

    gated_out = mixer_tok.astype(jnp.float32) * jax.nn.silu(gate_input.astype(jnp.float32))
    grouped = gated_out.reshape(gated_out.shape[0], gated_out.shape[1], groups, -1)
    norm_scale = lax.rsqrt(jnp.mean(grouped * grouped, axis=-1, keepdims=True) + EPS)
    normed = (grouped * norm_scale).reshape(gated_out.shape) * norm_gain
    return normed.astype(jnp.bfloat16)


def solution(mesh):
    n_tok, n_mlp = mesh.shape["tok"], mesh.shape["mlp"]
    split = Mesh(mesh.devices.reshape(GROUPS, n_tok // GROUPS, n_mlp), ("tz", "txc", "mlp"))
    tok = ("tz", "txc")
    return jax.shard_map(
        per_device,
        mesh=split,
        in_specs=(
            P(None, (*tok, "mlp"), None),
            P(None, (*tok, "mlp"), None),
            P(None, (*tok, "mlp"), None, None),
            P("mlp", None, tok),
            P(tok),
            P("mlp", None, tok),
            P("mlp", None, tok, None),
            P("mlp", tok, None),
            P("mlp"),
            P("mlp", None),
            P("mlp"),
            P(),
        ),
        out_specs=P(None, (*tok, "mlp"), None),
        check_vma=False,
    )
```

```python
import jax
import jax.numpy as jnp
from jax import lax
from jax.sharding import Mesh, PartitionSpec as P

EPS = 1e-05
GROUPS = 8


def per_device(
    new_x,
    gate_input,
    state_proj,
    step_size,
    decay_rate,
    x_cache,
    b_cache,
    decay_cache,
    lengths,
    sink_pos,
    windows,
    norm_gain,
):
    n_tz = lax.axis_size("tz")
    n_txc = lax.axis_size("txc")
    n_tok = n_tz * n_txc
    n_mlp = lax.axis_size("mlp")
    n_dev = n_tok * n_mlp
    groups = state_proj.shape[2]
    state_dim = b_cache.shape[3]
    heads_dev = decay_rate.shape[0]
    requests = step_size.shape[0]
    new_len = step_size.shape[1]
    tok_blk = new_x.shape[1]
    cache_len = x_cache.shape[1]
    chans = x_cache.shape[2]
    head_dim = chans // heads_dev

    part_b = lax.all_to_all(b_cache, "tz", split_axis=1, concat_axis=1, tiled=True)
    shared_b = lax.all_gather(part_b, "txc", axis=2)
    shared_b = shared_b.reshape(requests, cache_len, state_dim)

    sp = state_proj.reshape(n_mlp, requests, tok_blk, groups, 2 * state_dim)
    sp = sp.transpose(3, 0, 1, 2, 4).reshape(groups * n_mlp, requests, tok_blk, -1)
    sp = lax.all_to_all(sp, ("tz", "mlp"), 0, 0, tiled=True)
    sp = lax.all_gather(sp, "txc", axis=1)
    sp = sp.reshape(n_tz, n_mlp, n_txc, requests, tok_blk, -1).transpose(3, 0, 2, 1, 4, 5)
    sp = sp.reshape(requests, new_len, -1)
    b_new = sp[..., :state_dim]
    c_now = sp[..., state_dim:]

    x_part = new_x.reshape(n_mlp, requests, tok_blk, n_tok, chans).transpose(3, 0, 1, 2, 4)
    x_part = x_part.reshape(n_dev, requests, tok_blk, chans)
    head_x = lax.all_to_all(x_part, ("tz", "txc", "mlp"), 0, 0, tiled=True)
    head_x = head_x.transpose(1, 0, 2, 3).reshape(requests, new_len, chans)

    head_decay_values = jnp.exp(decay_rate)
    cum_new = jnp.cumsum(-(step_size * head_decay_values), axis=1)
    scaled = head_x.astype(jnp.float32).reshape(requests, new_len, heads_dev, head_dim)
    scaled = (scaled * step_size[..., None]).astype(jnp.bfloat16)

    positions = jnp.arange(cache_len, dtype=jnp.int32)
    token_order = jnp.arange(new_len, dtype=jnp.int32)
    live = positions[None, :] < lengths[:, None]
    masked = jnp.where(live[:, None, :], decay_cache, 0.0)
    local_sum = jnp.cumsum(masked, axis=2)
    tail_sum = local_sum[:, :, -1:] - local_sum

    col_scale = jnp.exp(tail_sum)
    row_scale = jnp.exp(cum_new)
    x_scaled = x_cache.astype(jnp.float32).reshape(requests, cache_len, heads_dev, head_dim)
    x_scaled = x_scaled * col_scale.transpose(0, 2, 1)[..., None]
    x_scaled = x_scaled.reshape(requests, cache_len, chans)
    x_pair = x_scaled.astype(jnp.bfloat16)

    query_pos = lengths[:, None] + token_order[None, :]
    score_new = jnp.einsum("rnk,rjk->rnj", c_now, b_new, preferred_element_type=jnp.float32)
    new_gap = token_order[:, None] - token_order[None, :]
    keep_new = (new_gap[None] >= 0) & (new_gap[None] < windows[:, None, None])
    cum_t = cum_new.transpose(0, 2, 1)
    decay_new = jnp.exp(jnp.minimum(cum_t[:, :, :, None] - cum_t[:, :, None, :], 0.0))
    weight_new = jnp.where(keep_new[:, None], decay_new, 0.0)
    probs_new = (score_new[:, None] * weight_new).astype(jnp.bfloat16)
    new_out = jnp.einsum("rhnj,rjhd->rnhd", probs_new, scaled, preferred_element_type=jnp.float32)


    new_out, x_pair, shared_b = lax.optimization_barrier((new_out, x_pair, shared_b))

    in_window = (query_pos[:, :, None] - positions[None, None, :] < windows[:, None, None]) & live[
        :, None, :
    ]
    score_old = jnp.einsum("rnk,rsk->rns", c_now, shared_b, preferred_element_type=jnp.float32)
    probs_old = jnp.where(in_window, score_old, 0.0).astype(jnp.bfloat16)
    acc = jnp.einsum("rns,rsc->rnc", probs_old, x_pair, preferred_element_type=jnp.float32)
    old_out = acc.reshape(requests, new_len, heads_dev, head_dim)
    old_out = old_out * row_scale[..., None]

    sink_b = jnp.take_along_axis(shared_b, sink_pos[:, :, None], axis=1)
    sink_x = jnp.take_along_axis(x_cache, sink_pos[:, :, None], axis=1)
    sink_live = sink_pos < lengths[:, None]
    sink_gap = query_pos[:, :, None] - sink_pos[:, None, :]
    sink_only = sink_live[:, None, :] & jnp.logical_not(sink_gap < windows[:, None, None])
    score_sink = jnp.einsum("rnk,rjk->rnj", c_now, sink_b, preferred_element_type=jnp.float32)
    probs_sink = jnp.where(sink_only, score_sink, 0.0).astype(jnp.bfloat16)
    sink_out = jnp.einsum("rnj,rjc->rnc", probs_sink, sink_x, preferred_element_type=jnp.float32)

    mixer_out = (old_out + new_out).reshape(requests, new_len, chans) + sink_out
    mixer_out = mixer_out.astype(jnp.bfloat16)

    back = mixer_out.reshape(requests, n_dev, tok_blk, chans).transpose(1, 0, 2, 3)
    back = lax.all_to_all(back, ("tz", "txc", "mlp"), 0, 0, tiled=True)
    back = back.reshape(n_tz, n_txc, n_mlp, requests, tok_blk, chans)

    gate = gate_input.reshape(n_mlp, requests, tok_blk, n_tz, n_txc, chans)
    gate = gate.transpose(3, 4, 0, 1, 2, 5).astype(jnp.float32)
    gated_out = back.astype(jnp.float32) * jax.nn.silu(gate)
    norm_scale = lax.rsqrt(jnp.mean(gated_out * gated_out, axis=(1, 5), keepdims=True) + EPS)
    gain = norm_gain.reshape(n_tz, n_txc, 1, 1, 1, chans)
    normed = (gated_out * norm_scale * gain).astype(jnp.bfloat16)
    normed = normed.transpose(2, 3, 4, 0, 1, 5)
    return normed.reshape(n_mlp * requests, tok_blk, n_tok * chans)


def solution(mesh):
    n_tok, n_mlp = mesh.shape["tok"], mesh.shape["mlp"]
    split = Mesh(mesh.devices.reshape(GROUPS, n_tok // GROUPS, n_mlp), ("tz", "txc", "mlp"))
    tok = ("tz", "txc")
    return jax.shard_map(
        per_device,
        mesh=split,
        in_specs=(
            P(None, (*tok, "mlp"), None),
            P(None, (*tok, "mlp"), None),
            P(None, (*tok, "mlp"), None, None),
            P("mlp", None, tok),
            P(tok),
            P("mlp", None, tok),
            P("mlp", None, tok, None),
            P("mlp", tok, None),
            P("mlp"),
            P("mlp", None),
            P("mlp"),
            P(),
        ),
        out_specs=P(None, (*tok, "mlp"), None),
        check_vma=False,
    )
```

```python
import jax
import jax.numpy as jnp
from jax import lax
from jax.sharding import Mesh, PartitionSpec as P

EPS = 1e-05
GROUPS = 8


def per_device(
    new_x,
    gate_input,
    state_proj,
    step_size,
    decay_rate,
    x_cache,
    b_cache,
    decay_cache,
    lengths,
    sink_pos,
    windows,
    norm_gain,
):
    n_tz = lax.axis_size("tz")
    n_txc = lax.axis_size("txc")
    n_tok = n_tz * n_txc
    n_mlp = lax.axis_size("mlp")
    n_dev = n_tok * n_mlp
    groups = state_proj.shape[2]
    state_dim = b_cache.shape[3]
    heads_dev = decay_rate.shape[0]
    requests = step_size.shape[0]
    new_len = step_size.shape[1]
    tok_blk = new_x.shape[1]
    cache_len = x_cache.shape[1]
    chans = x_cache.shape[2]
    head_dim = chans // heads_dev

    part_b = lax.all_to_all(b_cache, "tz", split_axis=1, concat_axis=1, tiled=True)
    shared_b = lax.all_gather(part_b, "txc", axis=2)
    shared_b = shared_b.reshape(requests, cache_len, state_dim)

    sp = state_proj.reshape(n_mlp, requests, tok_blk, groups, 2 * state_dim)
    sp = sp.transpose(3, 0, 1, 2, 4).reshape(groups * n_mlp, requests, tok_blk, -1)
    sp = lax.all_to_all(sp, ("tz", "mlp"), 0, 0, tiled=True)
    sp = lax.all_gather(sp, "txc", axis=1)
    sp = sp.reshape(n_tz, n_mlp, n_txc, requests, tok_blk, -1).transpose(3, 0, 2, 1, 4, 5)
    sp = sp.reshape(requests, new_len, -1)
    b_new = sp[..., :state_dim]
    c_now = sp[..., state_dim:]

    x_part = new_x.reshape(n_mlp, requests, tok_blk, n_tok, chans).transpose(3, 0, 1, 2, 4)
    x_part = x_part.reshape(n_dev, requests, tok_blk, chans)
    head_x = lax.all_to_all(x_part, ("tz", "txc", "mlp"), 0, 0, tiled=True)
    head_x = head_x.transpose(1, 0, 2, 3).reshape(requests, new_len, chans)

    head_decay_values = jnp.exp(decay_rate)
    cum_new = jnp.cumsum(-(step_size * head_decay_values), axis=1)
    scaled = head_x.astype(jnp.float32).reshape(requests, new_len, heads_dev, head_dim)
    scaled = (scaled * step_size[..., None]).astype(jnp.bfloat16)

    positions = jnp.arange(cache_len, dtype=jnp.int32)
    token_order = jnp.arange(new_len, dtype=jnp.int32)
    live = positions[None, :] < lengths[:, None]
    masked = jnp.where(live[:, None, :], decay_cache, 0.0)
    local_sum = jnp.cumsum(masked, axis=2)
    tail_sum = local_sum[:, :, -1:] - local_sum

    col_scale = jnp.exp(tail_sum)
    row_scale = jnp.exp(cum_new)
    x_scaled = x_cache.astype(jnp.float32).reshape(requests, cache_len, heads_dev, head_dim)
    x_scaled = x_scaled * col_scale.transpose(0, 2, 1)[..., None]
    x_scaled = x_scaled.reshape(requests, cache_len, chans)
    x_pair = x_scaled.astype(jnp.bfloat16)

    query_pos = lengths[:, None] + token_order[None, :]
    score_new = jnp.einsum("rnk,rjk->rnj", c_now, b_new, preferred_element_type=jnp.float32)
    new_gap = token_order[:, None] - token_order[None, :]
    keep_new = (new_gap[None] >= 0) & (new_gap[None] < windows[:, None, None])
    cum_t = cum_new.transpose(0, 2, 1)
    decay_new = jnp.exp(jnp.minimum(cum_t[:, :, :, None] - cum_t[:, :, None, :], 0.0))
    weight_new = jnp.where(keep_new[:, None], decay_new, 0.0)
    probs_new = (score_new[:, None] * weight_new).astype(jnp.bfloat16)
    new_out = jnp.einsum("rhnj,rjhd->rnhd", probs_new, scaled, preferred_element_type=jnp.float32)


    new_out, x_pair, shared_b = lax.optimization_barrier((new_out, x_pair, shared_b))

    in_window = (query_pos[:, :, None] - positions[None, None, :] < windows[:, None, None]) & live[
        :, None, :
    ]
    score_old = jnp.einsum("rnk,rsk->rns", c_now, shared_b, preferred_element_type=jnp.float32)
    probs_old = jnp.where(in_window, score_old, 0.0).astype(jnp.bfloat16)
    acc = jnp.einsum("rns,rsc->rnc", probs_old, x_pair, preferred_element_type=jnp.float32)
    old_out = acc.reshape(requests, new_len, heads_dev, head_dim)
    old_out = old_out * row_scale[..., None]

    sink_b = jnp.take_along_axis(shared_b, sink_pos[:, :, None], axis=1)
    sink_x = jnp.take_along_axis(x_cache, sink_pos[:, :, None], axis=1)
    sink_live = sink_pos < lengths[:, None]
    sink_gap = query_pos[:, :, None] - sink_pos[:, None, :]
    sink_only = sink_live[:, None, :] & jnp.logical_not(sink_gap < windows[:, None, None])
    score_sink = jnp.einsum("rnk,rjk->rnj", c_now, sink_b, preferred_element_type=jnp.float32)
    probs_sink = jnp.where(sink_only, score_sink, 0.0).astype(jnp.bfloat16)
    sink_out = jnp.einsum("rnj,rjc->rnc", probs_sink, sink_x, preferred_element_type=jnp.float32)

    mixer_out = (old_out + new_out).reshape(requests, new_len, chans) + sink_out
    mixer_out = mixer_out.astype(jnp.bfloat16)

    back = mixer_out.reshape(requests, n_dev, tok_blk, chans).transpose(1, 0, 2, 3)
    back = lax.all_to_all(back, ("tz", "txc", "mlp"), 0, 0, tiled=True)
    back = back.reshape(n_tok, n_mlp, requests, tok_blk, chans).transpose(1, 2, 3, 0, 4)
    mixer_tok = back.reshape(n_mlp * requests, tok_blk, n_tok * chans)

    gated_out = mixer_tok.astype(jnp.float32) * jax.nn.silu(gate_input.astype(jnp.float32))
    grouped = gated_out.reshape(gated_out.shape[0], gated_out.shape[1], groups, -1)
    norm_scale = lax.rsqrt(jnp.mean(grouped * grouped, axis=-1, keepdims=True) + EPS)
    normed = (grouped * norm_scale).reshape(gated_out.shape) * norm_gain
    return normed.astype(jnp.bfloat16)


def solution(mesh):
    n_tok, n_mlp = mesh.shape["tok"], mesh.shape["mlp"]
    split = Mesh(mesh.devices.reshape(GROUPS, n_tok // GROUPS, n_mlp), ("tz", "txc", "mlp"))
    tok = ("tz", "txc")
    return jax.shard_map(
        per_device,
        mesh=split,
        in_specs=(
            P(None, (*tok, "mlp"), None),
            P(None, (*tok, "mlp"), None),
            P(None, (*tok, "mlp"), None, None),
            P("mlp", None, tok),
            P(tok),
            P("mlp", None, tok),
            P("mlp", None, tok, None),
            P("mlp", tok, None),
            P("mlp"),
            P("mlp", None),
            P("mlp"),
            P(),
        ),
        out_specs=P(None, (*tok, "mlp"), None),
        check_vma=False,
    )
```

```python
import jax
import jax.numpy as jnp
from jax import lax
from jax.sharding import Mesh, PartitionSpec as P

EPS = 1e-05
GROUPS = 8


def per_device(
    new_x,
    gate_input,
    state_proj,
    step_size,
    decay_rate,
    x_cache,
    b_cache,
    decay_cache,
    lengths,
    sink_pos,
    windows,
    norm_gain,
):
    n_tz = lax.axis_size("tz")
    n_txc = lax.axis_size("txc")
    n_tok = n_tz * n_txc
    n_mlp = lax.axis_size("mlp")
    n_dev = n_tok * n_mlp
    groups = state_proj.shape[2]
    state_dim = b_cache.shape[3]
    heads_dev = decay_rate.shape[0]
    requests = step_size.shape[0]
    new_len = step_size.shape[1]
    tok_blk = new_x.shape[1]
    cache_len = x_cache.shape[1]
    chans = x_cache.shape[2]
    head_dim = chans // heads_dev

    part_b = lax.all_to_all(b_cache, "tz", split_axis=1, concat_axis=1, tiled=True)
    shared_b = lax.all_gather(part_b, "txc", axis=2)
    shared_b = shared_b.reshape(requests, cache_len, state_dim)

    sp = state_proj.reshape(n_mlp, requests, tok_blk, groups, 2 * state_dim)
    sp = sp.transpose(3, 0, 1, 2, 4).reshape(groups * n_mlp, requests, tok_blk, -1)
    sp = lax.all_to_all(sp, ("tz", "mlp"), 0, 0, tiled=True)
    sp = lax.all_gather(sp, "txc", axis=1)
    sp = sp.reshape(n_tz, n_mlp, n_txc, requests, tok_blk, -1).transpose(3, 0, 2, 1, 4, 5)
    sp = sp.reshape(requests, new_len, -1)
    b_new = sp[..., :state_dim]
    c_now = sp[..., state_dim:]

    x_part = new_x.reshape(n_mlp, requests, tok_blk, n_tok, chans).transpose(3, 0, 1, 2, 4)
    x_part = x_part.reshape(n_dev, requests, tok_blk, chans)
    x_part, sp = lax.optimization_barrier((x_part, sp))
    head_x = lax.all_to_all(x_part, ("tz", "txc", "mlp"), 0, 0, tiled=True)
    head_x = head_x.transpose(1, 0, 2, 3).reshape(requests, new_len, chans)

    head_decay_values = jnp.exp(decay_rate)
    cum_new = jnp.cumsum(-(step_size * head_decay_values), axis=1)
    scaled = head_x.astype(jnp.float32).reshape(requests, new_len, heads_dev, head_dim)
    scaled = (scaled * step_size[..., None]).astype(jnp.bfloat16)

    positions = jnp.arange(cache_len, dtype=jnp.int32)
    token_order = jnp.arange(new_len, dtype=jnp.int32)
    live = positions[None, :] < lengths[:, None]
    masked = jnp.where(live[:, None, :], decay_cache, 0.0)
    local_sum = jnp.cumsum(masked, axis=2)
    tail_sum = local_sum[:, :, -1:] - local_sum

    col_scale = jnp.exp(tail_sum)
    row_scale = jnp.exp(cum_new)
    x_scaled = x_cache.astype(jnp.float32).reshape(requests, cache_len, heads_dev, head_dim)
    x_scaled = x_scaled * col_scale.transpose(0, 2, 1)[..., None]
    x_scaled = x_scaled.reshape(requests, cache_len, chans)
    x_pair = x_scaled.astype(jnp.bfloat16)

    query_pos = lengths[:, None] + token_order[None, :]
    score_new = jnp.einsum("rnk,rjk->rnj", c_now, b_new, preferred_element_type=jnp.float32)
    new_gap = token_order[:, None] - token_order[None, :]
    keep_new = (new_gap[None] >= 0) & (new_gap[None] < windows[:, None, None])
    cum_t = cum_new.transpose(0, 2, 1)
    decay_new = jnp.exp(jnp.minimum(cum_t[:, :, :, None] - cum_t[:, :, None, :], 0.0))
    weight_new = jnp.where(keep_new[:, None], decay_new, 0.0)
    probs_new = (score_new[:, None] * weight_new).astype(jnp.bfloat16)
    new_out = jnp.einsum("rhnj,rjhd->rnhd", probs_new, scaled, preferred_element_type=jnp.float32)


    new_out, x_pair, shared_b = lax.optimization_barrier((new_out, x_pair, shared_b))

    in_window = (query_pos[:, :, None] - positions[None, None, :] < windows[:, None, None]) & live[
        :, None, :
    ]
    score_old = jnp.einsum("rnk,rsk->rns", c_now, shared_b, preferred_element_type=jnp.float32)
    probs_old = jnp.where(in_window, score_old, 0.0).astype(jnp.bfloat16)
    acc = jnp.einsum("rns,rsc->rnc", probs_old, x_pair, preferred_element_type=jnp.float32)
    old_out = acc.reshape(requests, new_len, heads_dev, head_dim)
    old_out = old_out * row_scale[..., None]

    sink_b = jnp.take_along_axis(shared_b, sink_pos[:, :, None], axis=1)
    sink_x = jnp.take_along_axis(x_cache, sink_pos[:, :, None], axis=1)
    sink_live = sink_pos < lengths[:, None]
    sink_gap = query_pos[:, :, None] - sink_pos[:, None, :]
    sink_only = sink_live[:, None, :] & jnp.logical_not(sink_gap < windows[:, None, None])
    score_sink = jnp.einsum("rnk,rjk->rnj", c_now, sink_b, preferred_element_type=jnp.float32)
    probs_sink = jnp.where(sink_only, score_sink, 0.0).astype(jnp.bfloat16)
    sink_out = jnp.einsum("rnj,rjc->rnc", probs_sink, sink_x, preferred_element_type=jnp.float32)

    mixer_out = (old_out + new_out).reshape(requests, new_len, chans) + sink_out
    mixer_out = mixer_out.astype(jnp.bfloat16)

    back = mixer_out.reshape(requests, n_dev, tok_blk, chans).transpose(1, 0, 2, 3)
    back = lax.all_to_all(back, ("tz", "txc", "mlp"), 0, 0, tiled=True)
    back = back.reshape(n_tok, n_mlp, requests, tok_blk, chans).transpose(1, 2, 3, 0, 4)
    mixer_tok = lax.optimization_barrier(back.reshape(n_mlp * requests, tok_blk, n_tok * chans))

    gated_out = mixer_tok.astype(jnp.float32) * jax.nn.silu(gate_input.astype(jnp.float32))
    grouped = gated_out.reshape(gated_out.shape[0], gated_out.shape[1], groups, -1)
    norm_scale = lax.rsqrt(jnp.mean(grouped * grouped, axis=-1, keepdims=True) + EPS)
    normed = (grouped * norm_scale).reshape(gated_out.shape) * norm_gain
    return normed.astype(jnp.bfloat16)


def solution(mesh):
    n_tok, n_mlp = mesh.shape["tok"], mesh.shape["mlp"]
    split = Mesh(mesh.devices.reshape(GROUPS, n_tok // GROUPS, n_mlp), ("tz", "txc", "mlp"))
    tok = ("tz", "txc")
    return jax.shard_map(
        per_device,
        mesh=split,
        in_specs=(
            P(None, (*tok, "mlp"), None),
            P(None, (*tok, "mlp"), None),
            P(None, (*tok, "mlp"), None, None),
            P("mlp", None, tok),
            P(tok),
            P("mlp", None, tok),
            P("mlp", None, tok, None),
            P("mlp", tok, None),
            P("mlp"),
            P("mlp", None),
            P("mlp"),
            P(),
        ),
        out_specs=P(None, (*tok, "mlp"), None),
        check_vma=False,
    )
```
